256 devices in a mesh: row: 8 (over x, core), col: 32 (over z, y).
Axes of the slice: x: 4, y: 4, z: 8, core: 2. Of those that a mesh axis runs over, the one named last changes fastest.
Arguments:
- leaf_rhs: bfloat16 [6144, 128, 512], P(('row', 'col')), may hold values from -6 to 6
- leaf_inverse: bfloat16 [6144, 128, 128], P(('row', 'col')), as said below
- leaf_link: bfloat16 [6144, 128, 128], P(('row', 'col')), may hold values from -0.109375 to 0.109375
- leaf_parent: int32 [6144], P(('row', 'col')), may hold values from 0 to 255, as said below
- node_rhs: bfloat16 [256, 128, 512], P(('row', 'col')), may hold values from -6 to 6
- node_inverse: bfloat16 [256, 128, 128], P(('row', 'col')), as said below
- node_link: bfloat16 [256, 128, 128], P(('row', 'col')), may hold values from -0.25 to 0.25
- node_parent: int32 [256], P('row'), may hold values from 0 to 63, as said below
- middle_rhs: bfloat16 [64, 128, 512], P('row'), may hold values from -6 to 6
- middle_inverse: bfloat16 [64, 128, 128], P('row'), as said below
- middle_link: bfloat16 [64, 128, 128], P('row'), may hold values from -0.125 to 0.125
- middle_parent: int32 [64], P('row'), may hold values from 0 to 3
- top_rhs: bfloat16 [4, 128, 512], replicated, may hold values from -6 to 6
- top_inverse: bfloat16 [4, 128, 128], replicated, as said below
Outputs:
- leaf_result: bfloat16 [6144, 128, 512], P(('row', 'col'))
- node_result: bfloat16 [256, 128, 512], P(('row', 'col'))
- middle_result: bfloat16 [64, 128, 512], P('row')
- top_result: bfloat16 [4, 128, 512], replicated
The draws below stay inside these ranges and needn't reach their ends.
Inputs may be any that keep to these rules, and one draw needn't show every extreme that they name: `leaf_parent`: the parent of a leaf held by the device at grid row r lies in block row r: it is r * 32 + c for some c below 32. `node_parent`: the parent of second-level supernode r * 32 + c is r * 8 + j for some j below 8. `leaf_inverse`: each block is lower triangular. `node_inverse`: each block is lower triangular. `middle_inverse`: each block is lower triangular. `top_inverse`: each block is lower triangular.
All inputs are finite; a program needn't handle non-finite values.
Results may differ from the reference program's by a relative error of at most 0.017.
Values may be sent and summed in bfloat16 or wider, within the bound.
No kernel may reach another device: no remote copies, remote signals or barrier semaphores. Data moves between devices by JAX's collectives and lax.ppermute only.
A program may use at most 128 MiB of HBM per device.

```python
import jax
import jax.numpy as jnp
from jax import lax

W = 128
R = 512
LEAF_DEV = 24
K2 = 8
K3 = 4
PEERS = 32
NODES = 256
LEAVES = 6144
MIDDLE = 64


def draw_inverse(key, count):
    lower_key, diag_key = jax.random.split(key)
    lower = jax.random.normal(lower_key, (count, W, W), jnp.float32) * W ** (-0.5)
    diagonal = jax.random.uniform(diag_key, (count, W), jnp.float32, 0.7, 1.3)
    strict = jnp.tril(jnp.ones((W, W), jnp.float32), -1)
    identity = jnp.eye(W, dtype=jnp.float32)
    return (lower * strict + identity * diagonal[:, None, :]).astype(jnp.bfloat16)


def draw_leaf_inverse(key, part):
    return draw_inverse(jax.random.fold_in(key, 11), LEAVES)


def draw_node_inverse(key, part):
    return draw_inverse(jax.random.fold_in(key, 12), NODES)


def draw_middle_inverse(key, part):
    return draw_inverse(jax.random.fold_in(key, 13), MIDDLE)


def draw_top_inverse(key, part):
    return draw_inverse(jax.random.fold_in(key, 14), K3)


def draw_leaf_parent(key, part):
    chosen = jax.random.randint(jax.random.fold_in(key, 21), (LEAVES,), 0, PEERS)
    grid_row = jnp.arange(LEAVES, dtype=jnp.int32) // (LEAF_DEV * PEERS)
    return (grid_row * PEERS + chosen).astype(jnp.int32)


def draw_node_parent(key, part):
    chosen = jax.random.randint(jax.random.fold_in(key, 22), (NODES,), 0, K2)
    grid_row = jnp.arange(NODES, dtype=jnp.int32) // PEERS
    return (grid_row * K2 + chosen).astype(jnp.int32)


def set_ends(result, rng, least, largest):
    extent = result.shape
    place = [jax.random.randint(jax.random.fold_in(rng, axis), (), 0, extent[axis]) for axis in range(len(extent))]
    result = result.at[tuple(place)].set(least)
    longest = extent.index(max(extent))
    place[longest] = (place[longest] + 1) % extent[longest]
    return result.at[tuple(place)].set(largest)


def levels(stream_key, dims, cuts, smallest, top_value):
    level, own = 1.0, jax.random.fold_in(stream_key, 6)
    for axis_at, blocks in cuts:
        steps = jnp.exp(jax.random.uniform(jax.random.fold_in(own, axis_at), (blocks,), jnp.float32, smallest / len(cuts), top_value / len(cuts)))
        level = level * jnp.repeat(steps, dims[axis_at] // blocks).reshape([-1 if axis == axis_at else 1 for axis in range(len(dims))])
    return level


def centred(rng, shape, scale, most, cuts=(), held_as=jnp.bfloat16):
    level = levels(rng, shape, cuts, -0.22, 0.18) if cuts else 1.0
    values = jax.random.normal(rng, shape, jnp.float32) * scale * level
    return jnp.minimum(jnp.maximum(values, -most), most).astype(held_as)


def setup_inputs(seed: int = 0) -> dict:
    arg_keys = jax.random.split(jax.random.key(seed), 15)
    leaf_rhs = centred(arg_keys[0], (LEAVES, W, R), 1.0, 6.0, ((0, 256),))
    leaf_inverse = draw_leaf_inverse(jax.random.fold_in(arg_keys[14], 71), 0)
    leaf_link = centred(arg_keys[2], (LEAVES, W, W), (W * LEAF_DEV) ** -0.5, 0.109375, ((0, 256),))
    leaf_parent = draw_leaf_parent(jax.random.fold_in(arg_keys[14], 71), 0)
    node_rhs = centred(arg_keys[4], (NODES, W, R), 1.0, 6.0, ((0, 256),))
    node_inverse = draw_node_inverse(jax.random.fold_in(arg_keys[14], 71), 0)
    node_link = centred(arg_keys[6], (NODES, W, W), (W * PEERS // K2) ** -0.5, 0.25, ((0, 256),))
    node_parent = draw_node_parent(jax.random.fold_in(arg_keys[14], 71), 0)
    middle_rhs = centred(arg_keys[8], (MIDDLE, W, R), 1.0, 6.0, ((0, 8),))
    middle_inverse = draw_middle_inverse(jax.random.fold_in(arg_keys[14], 71), 0)
    middle_link = centred(arg_keys[10], (MIDDLE, W, W), (W * MIDDLE // K3) ** -0.5, 0.125, ((0, 8),))
    middle_parent = set_ends(jax.random.randint(arg_keys[11], (MIDDLE,), 0, K3), jax.random.fold_in(arg_keys[11], 1), 0, K3 - 1).astype(jnp.int32)
    top_rhs = centred(arg_keys[12], (K3, W, R), 1.0, 6.0)
    top_inverse = draw_top_inverse(jax.random.fold_in(arg_keys[14], 71), 0)
    return {"leaf_rhs": leaf_rhs, "leaf_inverse": leaf_inverse, "leaf_link": leaf_link, "leaf_parent": leaf_parent, "node_rhs": node_rhs, "node_inverse": node_inverse, "node_link": node_link, "node_parent": node_parent, "middle_rhs": middle_rhs, "middle_inverse": middle_inverse, "middle_link": middle_link, "middle_parent": middle_parent, "top_rhs": top_rhs, "top_inverse": top_inverse}


def apply_block(matrix, vectors):
    return jnp.einsum("nij,njr->nir", matrix.astype(jnp.float32), vectors.astype(jnp.float32), precision=lax.Precision.HIGHEST)


def apply_transposed(matrix, vectors):
    return jnp.einsum("nij,nir->njr", matrix.astype(jnp.float32), vectors.astype(jnp.float32), precision=lax.Precision.HIGHEST)


def reference(leaf_rhs, leaf_inverse, leaf_link, leaf_parent, node_rhs, node_inverse, node_link, node_parent, middle_rhs, middle_inverse, middle_link, middle_parent, top_rhs, top_inverse):
    blocks = leaf_rhs.shape[0] // LEAF_DEV
    width = leaf_rhs.shape[1]
    columns = leaf_rhs.shape[2]
    items = (leaf_rhs.reshape(blocks, LEAF_DEV, width, columns), leaf_inverse.reshape(blocks, LEAF_DEV, width, width), leaf_link.reshape(blocks, LEAF_DEV, width, width), leaf_parent.reshape(blocks, LEAF_DEV))

    def forward_block(total, item):
        rhs, inverse, link, parent = item
        solved = apply_block(inverse, rhs).astype(jnp.bfloat16)
        update = apply_block(link, solved)
        total = total + jax.ops.segment_sum(update, parent, num_segments=NODES)
        return total, solved

    start = jnp.zeros((NODES, width, columns), jnp.float32)
    node_sum, leaf_solved = lax.scan(forward_block, start, items)
    node_y = (node_rhs.astype(jnp.float32) - node_sum).astype(jnp.bfloat16)
    node_solved = apply_block(node_inverse, node_y).astype(jnp.bfloat16)
    middle_sum = jax.ops.segment_sum(apply_block(node_link, node_solved), node_parent, num_segments=MIDDLE)
    middle_y = (middle_rhs.astype(jnp.float32) - middle_sum).astype(jnp.bfloat16)
    middle_solved = apply_block(middle_inverse, middle_y).astype(jnp.bfloat16)
    top_sum = jax.ops.segment_sum(apply_block(middle_link, middle_solved), middle_parent, num_segments=K3)
    top_y = (top_rhs.astype(jnp.float32) - top_sum).astype(jnp.bfloat16)
    top_solved = apply_block(top_inverse, top_y).astype(jnp.bfloat16)
    top_result = apply_transposed(top_inverse, top_solved).astype(jnp.bfloat16)
    middle_w = (middle_solved.astype(jnp.float32) - apply_transposed(middle_link, top_result[middle_parent])).astype(jnp.bfloat16)
    middle_result = apply_transposed(middle_inverse, middle_w).astype(jnp.bfloat16)
    node_w = (node_solved.astype(jnp.float32) - apply_transposed(node_link, middle_result[node_parent])).astype(jnp.bfloat16)
    node_result = apply_transposed(node_inverse, node_w).astype(jnp.bfloat16)

    def backward_block(item):
        solved, inverse, link, parent = item
        leaf_w = (solved.astype(jnp.float32) - apply_transposed(link, node_result[parent])).astype(jnp.bfloat16)
        return apply_transposed(inverse, leaf_w).astype(jnp.bfloat16)

    leaf_out = lax.map(backward_block, (leaf_solved, items[1], items[2], items[3]))
    leaf_result = leaf_out.reshape(blocks * LEAF_DEV, width, columns)
    return (leaf_result, node_result, middle_result, top_result)
```

```python
import jax
import jax.numpy as jnp
from jax import lax
from jax.sharding import PartitionSpec as P


def apply_block(matrix, vectors):
    return jnp.einsum("nij,njr->nir", matrix, vectors, preferred_element_type=jnp.float32)


def apply_transposed(matrix, vectors):
    return jnp.einsum("nij,nir->njr", matrix, vectors, preferred_element_type=jnp.float32)


def slot_sums(targets, count, values):
    slots = lax.iota(jnp.int32, count)
    select = (slots[:, None] == targets[None, :]).astype(jnp.float32)
    return jnp.einsum("sk,kwr->swr", select, values, precision=lax.Precision.HIGHEST)


def local(
    leaf_rhs,
    leaf_inverse,
    leaf_link,
    leaf_parent,
    node_rhs,
    node_inverse,
    node_link,
    node_parent,
    middle_rhs,
    middle_inverse,
    middle_link,
    middle_parent,
    top_rhs,
    top_inverse,
):
    peers = lax.axis_size("col")
    col_index = lax.axis_index("col")
    width = leaf_rhs.shape[1]
    columns = leaf_rhs.shape[2]
    chunk = columns // peers
    middle_count = middle_rhs.shape[0]
    top_count = top_rhs.shape[0]
    leaf_target = leaf_parent % peers
    middle_target = node_parent % middle_count

    leaf_solved = apply_block(leaf_inverse, leaf_rhs).astype(jnp.bfloat16)
    leaf_update = apply_block(leaf_link, leaf_solved)
    outgoing = slot_sums(leaf_target, peers, leaf_update).astype(jnp.bfloat16)
    incoming = lax.all_to_all(outgoing, "col", 0, 0, tiled=True)
    node_sum = jnp.sum(incoming.astype(jnp.float32), axis=0, keepdims=True)
    node_y = (node_rhs.astype(jnp.float32) - node_sum).astype(jnp.bfloat16)
    node_solved = apply_block(node_inverse, node_y).astype(jnp.bfloat16)

    node_update = apply_block(node_link, node_solved)[0]
    pieces = node_update.reshape(width, peers, chunk).transpose(1, 0, 2)
    row_updates = lax.all_to_all(pieces, "col", 0, 0, tiled=True)
    middle_sum = slot_sums(middle_target, middle_count, row_updates)
    start = col_index * chunk
    middle_piece = lax.dynamic_slice_in_dim(middle_rhs, start, chunk, 2)
    middle_y = (middle_piece.astype(jnp.float32) - middle_sum).astype(jnp.bfloat16)
    middle_solved = apply_block(middle_inverse, middle_y).astype(jnp.bfloat16)
    top_term = slot_sums(middle_parent, top_count, apply_block(middle_link, middle_solved))
    top_sum = lax.psum(top_term, "row")
    top_piece = lax.dynamic_slice_in_dim(top_rhs, start, chunk, 2)
    top_y = (top_piece.astype(jnp.float32) - top_sum).astype(jnp.bfloat16)
    top_solved = apply_block(top_inverse, top_y).astype(jnp.bfloat16)
    top_part = apply_transposed(top_inverse, top_solved).astype(jnp.bfloat16)
    middle_w = (
        middle_solved.astype(jnp.float32) - apply_transposed(middle_link, top_part[middle_parent])
    ).astype(jnp.bfloat16)
    middle_part = apply_transposed(middle_inverse, middle_w).astype(jnp.bfloat16)
    parts = jnp.concatenate([middle_part, top_part], axis=0)
    gathered = lax.all_gather(parts, "col", axis=0, tiled=False)
    whole = gathered.transpose(1, 2, 0, 3).reshape(middle_count + top_count, width, columns)
    middle_result = whole[:middle_count]
    top_result = whole[middle_count:]

    own_target = lax.dynamic_slice_in_dim(middle_target, col_index, 1)
    node_w = (
        node_solved.astype(jnp.float32) - apply_transposed(node_link, middle_result[own_target])
    ).astype(jnp.bfloat16)
    node_result = apply_transposed(node_inverse, node_w).astype(jnp.bfloat16)
    row_result = lax.all_gather(node_result, "col", axis=0, tiled=True)
    leaf_w = (
        leaf_solved.astype(jnp.float32) - apply_transposed(leaf_link, row_result[leaf_target])
    ).astype(jnp.bfloat16)
    leaf_result = apply_transposed(leaf_inverse, leaf_w).astype(jnp.bfloat16)
    return (leaf_result, node_result, middle_result, top_result)


def solution(mesh):
    placed = (
        P(("row", "col"), None, None),
        P(("row", "col"), None, None),
        P(("row", "col"), None, None),
        P(("row", "col")),
        P(("row", "col"), None, None),
        P(("row", "col"), None, None),
        P(("row", "col"), None, None),
        P("row"),
        P("row", None, None),
        P("row", None, None),
        P("row", None, None),
        P("row"),
        P(),
        P(),
    )
    return jax.shard_map(
        local,
        mesh=mesh,
        in_specs=placed,
        out_specs=(
            P(("row", "col"), None, None),
            P(("row", "col"), None, None),
            P("row", None, None),
            P(),
        ),
        check_vma=False,
    )
```

```python
import jax
import jax.numpy as jnp
from jax import lax
from jax.sharding import PartitionSpec as P


def apply_block(matrix, vectors):
    return jnp.einsum("nij,njr->nir", matrix, vectors, preferred_element_type=jnp.float32)


def apply_transposed(matrix, vectors):
    return jnp.einsum("nij,nir->njr", matrix, vectors, preferred_element_type=jnp.float32)


def piece_block(matrix, pieces):
    return jnp.einsum("nij,ncj->nci", matrix, pieces, preferred_element_type=jnp.float32)


def piece_transposed(matrix, pieces):
    return jnp.einsum("nij,nci->ncj", matrix, pieces, preferred_element_type=jnp.float32)


def slot_sums(targets, count, values):
    slots = lax.iota(jnp.int32, count)
    select = (slots[:, None] == targets[None, :]).astype(jnp.float32)
    return jnp.einsum("sk,k...->s...", select, values, precision=lax.Precision.HIGHEST)


def local(
    leaf_rhs,
    leaf_inverse,
    leaf_link,
    leaf_parent,
    node_rhs,
    node_inverse,
    node_link,
    node_parent,
    middle_rhs,
    middle_inverse,
    middle_link,
    middle_parent,
    top_rhs,
    top_inverse,
):
    peers = lax.axis_size("col")
    col_index = lax.axis_index("col")
    width = leaf_rhs.shape[1]
    columns = leaf_rhs.shape[2]
    chunk = columns // peers
    middle_count = middle_rhs.shape[0]
    top_count = top_rhs.shape[0]
    leaf_target = leaf_parent % peers
    middle_target = node_parent % middle_count
    start = col_index * chunk

    node_mats = lax.all_gather(jnp.concatenate([node_inverse, node_link], axis=0), "col", axis=0, tiled=False)
    row_inverse = node_mats[:, 0]
    row_link = node_mats[:, 1]

    leaf_solved = apply_block(leaf_inverse, leaf_rhs).astype(jnp.bfloat16)
    leaf_update = jnp.einsum("kij,kjr->kri", leaf_link, leaf_solved, preferred_element_type=jnp.float32)
    outgoing = jnp.concatenate(
        [slot_sums(leaf_target, peers, leaf_update).astype(jnp.bfloat16), node_rhs.transpose(0, 2, 1)], axis=0
    )
    outgoing = outgoing.reshape(peers + 1, peers, chunk, width).transpose(1, 0, 2, 3)
    incoming = lax.all_to_all(outgoing, "col", 0, 0, tiled=True)
    node_sum = jnp.sum(incoming[:, :peers].astype(jnp.float32), axis=0)
    node_y = (incoming[:, peers].astype(jnp.float32) - node_sum).astype(jnp.bfloat16)
    node_solved = piece_block(row_inverse, node_y).astype(jnp.bfloat16)
    middle_sum = slot_sums(middle_target, middle_count, piece_block(row_link, node_solved))
    middle_piece = lax.dynamic_slice_in_dim(middle_rhs, start, chunk, 2).transpose(0, 2, 1)
    middle_y = (middle_piece.astype(jnp.float32) - middle_sum).astype(jnp.bfloat16)
    middle_solved = piece_block(middle_inverse, middle_y).astype(jnp.bfloat16)
    top_term = slot_sums(middle_parent, top_count, piece_block(middle_link, middle_solved))
    top_sum = lax.psum(top_term, "row")
    top_piece = lax.dynamic_slice_in_dim(top_rhs, start, chunk, 2).transpose(0, 2, 1)
    top_y = (top_piece.astype(jnp.float32) - top_sum).astype(jnp.bfloat16)
    top_solved = piece_block(top_inverse, top_y).astype(jnp.bfloat16)
    top_part = piece_transposed(top_inverse, top_solved).astype(jnp.bfloat16)
    middle_w = (
        middle_solved.astype(jnp.float32) - piece_transposed(middle_link, top_part[middle_parent])
    ).astype(jnp.bfloat16)
    middle_part = piece_transposed(middle_inverse, middle_w).astype(jnp.bfloat16)
    node_w = (
        node_solved.astype(jnp.float32) - piece_transposed(row_link, middle_part[middle_target])
    ).astype(jnp.bfloat16)
    node_part = piece_transposed(row_inverse, node_w).astype(jnp.bfloat16)

    parts = jnp.concatenate([node_part, middle_part, top_part], axis=0)
    gathered = lax.all_gather(parts, "col", axis=0, tiled=False)
    whole = gathered.transpose(1, 3, 0, 2).reshape(parts.shape[0], width, columns)
    row_result = whole[:peers]
    middle_result = whole[peers : peers + middle_count]
    top_result = whole[peers + middle_count :]
    node_result = lax.dynamic_slice_in_dim(row_result, col_index, 1)

    leaf_w = (
        leaf_solved.astype(jnp.float32) - apply_transposed(leaf_link, row_result[leaf_target])
    ).astype(jnp.bfloat16)
    leaf_result = apply_transposed(leaf_inverse, leaf_w).astype(jnp.bfloat16)
    return (leaf_result, node_result, middle_result, top_result)


def solution(mesh):
    placed = (
        P(("row", "col"), None, None),
        P(("row", "col"), None, None),
        P(("row", "col"), None, None),
        P(("row", "col")),
        P(("row", "col"), None, None),
        P(("row", "col"), None, None),
        P(("row", "col"), None, None),
        P("row"),
        P("row", None, None),
        P("row", None, None),
        P("row", None, None),
        P("row"),
        P(),
        P(),
    )
    return jax.shard_map(
        local,
        mesh=mesh,
        in_specs=placed,
        out_specs=(
            P(("row", "col"), None, None),
            P(("row", "col"), None, None),
            P("row", None, None),
            P(),
        ),
        check_vma=False,
    )
```

```python
import jax
import jax.numpy as jnp
from jax import lax
from jax.sharding import Mesh
from jax.sharding import PartitionSpec as P

ROW = ("x", "core")
COL = ("z", "y")


def apply_block(matrix, vectors):
    return jnp.einsum("nij,njr->nir", matrix, vectors, preferred_element_type=jnp.float32)


def apply_transposed(matrix, vectors):
    return jnp.einsum("nij,nir->njr", matrix, vectors, preferred_element_type=jnp.float32)


def piece_block(matrix, pieces):
    return jnp.einsum("nij,ncj->nci", matrix, pieces, preferred_element_type=jnp.float32)


def piece_transposed(matrix, pieces):
    return jnp.einsum("nij,nci->ncj", matrix, pieces, preferred_element_type=jnp.float32)


def slot_sums(targets, count, values):
    slots = lax.iota(jnp.int32, count)
    select = (slots[:, None] == targets[None, :]).astype(jnp.float32)
    return jnp.einsum("sk,k...->s...", select, values, precision=lax.Precision.HIGHEST)


def local(
    leaf_rhs,
    leaf_inverse,
    leaf_link,
    leaf_parent,
    node_rhs,
    node_inverse,
    node_link,
    node_parent,
    middle_rhs,
    middle_inverse,
    middle_link,
    middle_parent,
    top_rhs,
    top_inverse,
):
    y_size = lax.axis_size("y")
    z_size = lax.axis_size("z")
    peers = y_size * z_size
    col_index = lax.axis_index(COL)
    width = leaf_rhs.shape[1]
    columns = leaf_rhs.shape[2]
    chunk = columns // peers
    middle_count = middle_rhs.shape[0]
    top_count = top_rhs.shape[0]
    leaf_target = leaf_parent % peers
    middle_target = node_parent % middle_count
    start = col_index * chunk

    node_mats = lax.all_gather(jnp.concatenate([node_inverse, node_link], axis=0), COL, axis=0, tiled=False)
    row_inverse = node_mats[:, 0]
    row_link = node_mats[:, 1]

    leaf_solved = apply_block(leaf_inverse, leaf_rhs).astype(jnp.bfloat16)
    leaf_update = jnp.einsum("kij,kjr->kri", leaf_link, leaf_solved, preferred_element_type=jnp.float32)
    outgoing = jnp.concatenate(
        [slot_sums(leaf_target, peers, leaf_update).astype(jnp.bfloat16), node_rhs.transpose(0, 2, 1)], axis=0
    )
    outgoing = outgoing.reshape(peers + 1, z_size, y_size, chunk, width).transpose(1, 2, 0, 3, 4)
    first = lax.all_to_all(outgoing, "y", 1, 1, tiled=True)
    partial = jnp.sum(first[:, :, :peers].astype(jnp.float32), axis=1).astype(jnp.bfloat16)
    second = jnp.concatenate([partial, first[:, :, peers]], axis=1)
    incoming = lax.all_to_all(second, "z", 0, 0, tiled=True)
    node_sum = jnp.sum(incoming[:, :peers].astype(jnp.float32), axis=0)
    own_rhs = incoming[:, peers:].reshape(peers, chunk, width)
    node_y = (own_rhs.astype(jnp.float32) - node_sum).astype(jnp.bfloat16)
    node_solved = piece_block(row_inverse, node_y).astype(jnp.bfloat16)
    middle_sum = slot_sums(middle_target, middle_count, piece_block(row_link, node_solved))
    middle_piece = lax.dynamic_slice_in_dim(middle_rhs, start, chunk, 2).transpose(0, 2, 1)
    middle_y = (middle_piece.astype(jnp.float32) - middle_sum).astype(jnp.bfloat16)
    middle_solved = piece_block(middle_inverse, middle_y).astype(jnp.bfloat16)
    top_term = slot_sums(middle_parent, top_count, piece_block(middle_link, middle_solved))
    top_sum = top_term
    rows = lax.axis_size(ROW)
    step = 1
    while step < rows:
        top_sum = top_sum + lax.ppermute(top_sum, ROW, [(i, i ^ step) for i in range(rows)])
        step *= 2
    top_piece = lax.dynamic_slice_in_dim(top_rhs, start, chunk, 2).transpose(0, 2, 1)
    top_y = (top_piece.astype(jnp.float32) - top_sum).astype(jnp.bfloat16)
    top_solved = piece_block(top_inverse, top_y).astype(jnp.bfloat16)
    top_part = piece_transposed(top_inverse, top_solved).astype(jnp.bfloat16)
    middle_w = (
        middle_solved.astype(jnp.float32) - piece_transposed(middle_link, top_part[middle_parent])
    ).astype(jnp.bfloat16)
    middle_part = piece_transposed(middle_inverse, middle_w).astype(jnp.bfloat16)
    node_w = (
        node_solved.astype(jnp.float32) - piece_transposed(row_link, middle_part[middle_target])
    ).astype(jnp.bfloat16)
    node_part = piece_transposed(row_inverse, node_w).astype(jnp.bfloat16)

    parts = jnp.concatenate([node_part, middle_part, top_part], axis=0)
    gathered = lax.all_gather(parts, COL, axis=0, tiled=False)
    whole = gathered.transpose(1, 3, 0, 2).reshape(parts.shape[0], width, columns)
    row_result = whole[:peers]
    middle_result = whole[peers : peers + middle_count]
    top_result = whole[peers + middle_count :]
    node_result = lax.dynamic_slice_in_dim(row_result, col_index, 1)

    leaf_w = (
        leaf_solved.astype(jnp.float32) - apply_transposed(leaf_link, row_result[leaf_target])
    ).astype(jnp.bfloat16)
    leaf_result = apply_transposed(leaf_inverse, leaf_w).astype(jnp.bfloat16)
    return (leaf_result, node_result, middle_result, top_result)


def solution(mesh):
    cores = len({d.core_on_chip for d in mesh.devices[:, 0]})
    y_size = len({d.coords[1] for d in mesh.devices[0]})
    grid = mesh.devices.reshape(mesh.shape["row"] // cores, cores, -1, y_size)
    view = Mesh(grid, ("x", "core", "z", "y"))
    placed = (
        P((*ROW, *COL), None, None),
        P((*ROW, *COL), None, None),
        P((*ROW, *COL), None, None),
        P((*ROW, *COL)),
        P((*ROW, *COL), None, None),
        P((*ROW, *COL), None, None),
        P((*ROW, *COL), None, None),
        P(ROW),
        P(ROW, None, None),
        P(ROW, None, None),
        P(ROW, None, None),
        P(ROW),
        P(),
        P(),
    )
    return jax.shard_map(
        local,
        mesh=view,
        in_specs=placed,
        out_specs=(
            P((*ROW, *COL), None, None),
            P((*ROW, *COL), None, None),
            P(ROW, None, None),
            P(),
        ),
        check_vma=False,
    )
```

```python
import jax
import jax.numpy as jnp
from jax import lax
from jax.sharding import Mesh
from jax.sharding import PartitionSpec as P

ROW = ("x", "core")
COL = ("z", "y")


def apply_block(matrix, vectors):
    return jnp.einsum("nij,njr->nir", matrix, vectors, preferred_element_type=jnp.float32)


def apply_transposed(matrix, vectors):
    return jnp.einsum("nij,nir->njr", matrix, vectors, preferred_element_type=jnp.float32)


def piece_block(matrix, pieces):
    return jnp.einsum("nij,ncj->nci", matrix, pieces, preferred_element_type=jnp.float32)


def piece_transposed(matrix, pieces):
    return jnp.einsum("nij,nci->ncj", matrix, pieces, preferred_element_type=jnp.float32)


def slot_sums(targets, count, values):
    slots = lax.iota(jnp.int32, count)
    select = (slots[:, None] == targets[None, :]).astype(jnp.float32)
    return jnp.einsum("sk,k...->s...", select, values, precision=lax.Precision.HIGHEST)


def local(
    leaf_rhs,
    leaf_inverse,
    leaf_link,
    leaf_parent,
    node_rhs,
    node_inverse,
    node_link,
    node_parent,
    middle_rhs,
    middle_inverse,
    middle_link,
    middle_parent,
    top_rhs,
    top_inverse,
):
    y_size = lax.axis_size("y")
    z_size = lax.axis_size("z")
    peers = y_size * z_size
    col_index = lax.axis_index(COL)
    width = leaf_rhs.shape[1]
    columns = leaf_rhs.shape[2]
    chunk = columns // peers
    middle_count = middle_rhs.shape[0]
    top_count = top_rhs.shape[0]
    leaf_target = leaf_parent % peers
    middle_target = node_parent % middle_count
    start = col_index * chunk

    node_mats = lax.all_gather(jnp.concatenate([node_inverse, node_link], axis=0), COL, axis=0, tiled=False)
    row_inverse = node_mats[:, 0]
    row_link = node_mats[:, 1]

    leaf_solved = apply_block(leaf_inverse, leaf_rhs).astype(jnp.bfloat16)
    leaf_update = jnp.einsum("kij,kjr->kri", leaf_link, leaf_solved, preferred_element_type=jnp.float32)
    outgoing = jnp.concatenate(
        [slot_sums(leaf_target, peers, leaf_update).astype(jnp.bfloat16), node_rhs.transpose(0, 2, 1)], axis=0
    )
    outgoing = outgoing.reshape(peers + 1, z_size, y_size, chunk, width).transpose(1, 2, 0, 3, 4)
    first = lax.all_to_all(outgoing, "y", 1, 1, tiled=True)
    partial = jnp.sum(first[:, :, :peers].astype(jnp.float32), axis=1).astype(jnp.bfloat16)
    second = jnp.concatenate([partial, first[:, :, peers]], axis=1)
    incoming = lax.all_to_all(second, "z", 0, 0, tiled=True)
    node_sum = jnp.sum(incoming[:, :peers].astype(jnp.float32), axis=0)
    own_rhs = incoming[:, peers:].reshape(peers, chunk, width)
    node_y = (own_rhs.astype(jnp.float32) - node_sum).astype(jnp.bfloat16)
    node_solved = piece_block(row_inverse, node_y).astype(jnp.bfloat16)
    middle_sum = slot_sums(middle_target, middle_count, piece_block(row_link, node_solved))
    middle_piece = lax.dynamic_slice_in_dim(middle_rhs, start, chunk, 2).transpose(0, 2, 1)
    middle_y = (middle_piece.astype(jnp.float32) - middle_sum).astype(jnp.bfloat16)
    middle_solved = piece_block(middle_inverse, middle_y).astype(jnp.bfloat16)
    top_term = slot_sums(middle_parent, top_count, piece_block(middle_link, middle_solved))
    top_sum = top_term
    rows = lax.axis_size(ROW)
    step = 1
    while step < rows:
        top_sum = top_sum + lax.ppermute(top_sum, ROW, [(i, i ^ step) for i in range(rows)])
        step *= 2
    top_piece = lax.dynamic_slice_in_dim(top_rhs, start, chunk, 2).transpose(0, 2, 1)
    top_y = (top_piece.astype(jnp.float32) - top_sum).astype(jnp.bfloat16)
    top_solved = piece_block(top_inverse, top_y).astype(jnp.bfloat16)
    top_part = piece_transposed(top_inverse, top_solved).astype(jnp.bfloat16)
    middle_w = (
        middle_solved.astype(jnp.float32) - piece_transposed(middle_link, top_part[middle_parent])
    ).astype(jnp.bfloat16)
    middle_part = piece_transposed(middle_inverse, middle_w).astype(jnp.bfloat16)
    node_w = (
        node_solved.astype(jnp.float32) - piece_transposed(row_link, middle_part[middle_target])
    ).astype(jnp.bfloat16)
    node_part = piece_transposed(row_inverse, node_w).astype(jnp.bfloat16)

    parts = jnp.concatenate([node_part, middle_part, top_part], axis=0)
    gathered = lax.all_gather(lax.all_gather(parts, "y", axis=0, tiled=False), "z", axis=0, tiled=True)
    upper = gathered[:, peers:].transpose(1, 3, 0, 2).reshape(middle_count + top_count, width, columns)
    middle_result = upper[:middle_count]
    top_result = upper[middle_count:]
    node_result = lax.dynamic_index_in_dim(gathered, col_index, 1).transpose(1, 3, 0, 2).reshape(1, width, columns)

    parent_t = gathered[:, leaf_target].transpose(1, 0, 2, 3).reshape(leaf_target.shape[0], columns, width)
    correction = jnp.einsum("kij,kci->kjc", leaf_link, parent_t, preferred_element_type=jnp.float32)
    leaf_w = (leaf_solved.astype(jnp.float32) - correction).astype(jnp.bfloat16)
    leaf_result = apply_transposed(leaf_inverse, leaf_w).astype(jnp.bfloat16)
    return (leaf_result, node_result, middle_result, top_result)


def solution(mesh):
    cores = len({d.core_on_chip for d in mesh.devices[:, 0]})
    y_size = len({d.coords[1] for d in mesh.devices[0]})
    grid = mesh.devices.reshape(mesh.shape["row"] // cores, cores, -1, y_size)
    view = Mesh(grid, ("x", "core", "z", "y"))
    placed = (
        P((*ROW, *COL), None, None),
        P((*ROW, *COL), None, None),
        P((*ROW, *COL), None, None),
        P((*ROW, *COL)),
        P((*ROW, *COL), None, None),
        P((*ROW, *COL), None, None),
        P((*ROW, *COL), None, None),
        P(ROW),
        P(ROW, None, None),
        P(ROW, None, None),
        P(ROW, None, None),
        P(ROW),
        P(),
        P(),
    )
    return jax.shard_map(
        local,
        mesh=view,
        in_specs=placed,
        out_specs=(
            P((*ROW, *COL), None, None),
            P((*ROW, *COL), None, None),
            P(ROW, None, None),
            P(),
        ),
        check_vma=False,
    )
```

```python
import jax
import jax.numpy as jnp
from jax import lax
from jax.sharding import Mesh
from jax.sharding import PartitionSpec as P

ROW = ("x", "core")
COL = ("z", "y")


def apply_block(matrix, vectors):
    return jnp.einsum("nij,njr->nir", matrix, vectors, preferred_element_type=jnp.float32)


def apply_transposed(matrix, vectors):
    return jnp.einsum("nij,nir->njr", matrix, vectors, preferred_element_type=jnp.float32)


def piece_block(matrix, pieces):
    return jnp.einsum("nij,ncj->nci", matrix, pieces, preferred_element_type=jnp.float32)


def piece_transposed(matrix, pieces):
    return jnp.einsum("nij,nci->ncj", matrix, pieces, preferred_element_type=jnp.float32)


def slot_sums(targets, count, values):
    slots = lax.iota(jnp.int32, count)
    select = (slots[:, None] == targets[None, :]).astype(jnp.float32)
    return jnp.einsum("sk,k...->s...", select, values, precision=lax.Precision.HIGHEST)


def split_slot_sums(targets, count, values):
    slots = lax.iota(jnp.int32, count)
    select = (slots[:, None] == targets[None, :]).astype(jnp.bfloat16)
    high = values.astype(jnp.bfloat16)
    low = (values - high.astype(jnp.float32)).astype(jnp.bfloat16)
    total = jnp.einsum("sk,k...->s...", select, high, preferred_element_type=jnp.float32)
    return total + jnp.einsum("sk,k...->s...", select, low, preferred_element_type=jnp.float32)


def local(
    leaf_rhs,
    leaf_inverse,
    leaf_link,
    leaf_parent,
    node_rhs,
    node_inverse,
    node_link,
    node_parent,
    middle_rhs,
    middle_inverse,
    middle_link,
    middle_parent,
    top_rhs,
    top_inverse,
):
    y_size = lax.axis_size("y")
    z_size = lax.axis_size("z")
    peers = y_size * z_size
    col_index = lax.axis_index(COL)
    width = leaf_rhs.shape[1]
    columns = leaf_rhs.shape[2]
    chunk = columns // peers
    middle_count = middle_rhs.shape[0]
    top_count = top_rhs.shape[0]
    leaf_target = leaf_parent % peers
    middle_target = node_parent % middle_count
    start = col_index * chunk

    node_mats = lax.all_gather(jnp.concatenate([node_inverse, node_link], axis=0), COL, axis=0, tiled=False)
    row_inverse = node_mats[:, 0]
    row_link = node_mats[:, 1]

    leaf_solved = apply_block(leaf_inverse, leaf_rhs).astype(jnp.bfloat16)
    leaf_update = jnp.einsum("kij,kjr->kri", leaf_link, leaf_solved, preferred_element_type=jnp.float32)
    half = peers // 2
    y_index = lax.axis_index("y")
    rhs_t = node_rhs.transpose(0, 2, 1)
    sums = []
    for group in range(2):
        targets = leaf_target - group * half
        entries = split_slot_sums(targets, half, leaf_update).astype(jnp.bfloat16)
        if group == 1:
            entries = jnp.concatenate([entries, rhs_t], axis=0)
        count = entries.shape[0]
        entries = entries.reshape(count, z_size, y_size, chunk, width).transpose(2, 1, 0, 3, 4)
        arrivals = [lax.dynamic_index_in_dim(entries, y_index, 0, keepdims=False)]
        for shift in range(1, y_size):
            outbound = lax.dynamic_index_in_dim(entries, (y_index + shift) % y_size, 0, keepdims=False)
            pairs = [(i, (i + shift) % y_size) for i in range(y_size)]
            arrivals.append(lax.ppermute(outbound, "y", pairs))
        partial = sum(a[:, :half].astype(jnp.float32) for a in arrivals).astype(jnp.bfloat16)
        if group == 1:
            partial = jnp.concatenate([partial, jnp.stack([a[:, half] for a in arrivals], axis=1)], axis=1)
        incoming = lax.all_to_all(partial, "z", 0, 0, tiled=True)
        sums.append(jnp.sum(incoming[:, :half].astype(jnp.float32), axis=0))
    node_sum = jnp.concatenate(sums, axis=0)
    offsets = (y_index - lax.iota(jnp.int32, y_size)) % y_size
    own_rhs = jnp.take(incoming[:, half:], offsets, axis=1).reshape(peers, chunk, width)
    node_y = (own_rhs.astype(jnp.float32) - node_sum).astype(jnp.bfloat16)
    node_solved = piece_block(row_inverse, node_y).astype(jnp.bfloat16)
    middle_sum = slot_sums(middle_target, middle_count, piece_block(row_link, node_solved))
    middle_piece = lax.dynamic_slice_in_dim(middle_rhs, start, chunk, 2).transpose(0, 2, 1)
    middle_y = (middle_piece.astype(jnp.float32) - middle_sum).astype(jnp.bfloat16)
    middle_solved = piece_block(middle_inverse, middle_y).astype(jnp.bfloat16)
    top_term = slot_sums(middle_parent, top_count, piece_block(middle_link, middle_solved))
    top_sum = top_term
    rows = lax.axis_size(ROW)
    step = 1
    while step < rows:
        top_sum = top_sum + lax.ppermute(top_sum, ROW, [(i, i ^ step) for i in range(rows)])
        step *= 2
    top_piece = lax.dynamic_slice_in_dim(top_rhs, start, chunk, 2).transpose(0, 2, 1)
    top_y = (top_piece.astype(jnp.float32) - top_sum).astype(jnp.bfloat16)
    top_solved = piece_block(top_inverse, top_y).astype(jnp.bfloat16)
    top_part = piece_transposed(top_inverse, top_solved).astype(jnp.bfloat16)
    middle_w = (
        middle_solved.astype(jnp.float32) - piece_transposed(middle_link, top_part[middle_parent])
    ).astype(jnp.bfloat16)
    middle_part = piece_transposed(middle_inverse, middle_w).astype(jnp.bfloat16)
    node_w = (
        node_solved.astype(jnp.float32) - piece_transposed(row_link, middle_part[middle_target])
    ).astype(jnp.bfloat16)
    node_part = piece_transposed(row_inverse, node_w).astype(jnp.bfloat16)

    parts = jnp.concatenate([node_part, middle_part, top_part], axis=0)
    gathered = lax.all_gather(lax.all_gather(parts, "y", axis=0, tiled=False), "z", axis=0, tiled=True)
    upper = gathered[:, peers:].transpose(1, 3, 0, 2).reshape(middle_count + top_count, width, columns)
    middle_result = upper[:middle_count]
    top_result = upper[middle_count:]
    node_result = lax.dynamic_index_in_dim(gathered, col_index, 1).transpose(1, 3, 0, 2).reshape(1, width, columns)

    parent_t = gathered[:, leaf_target].transpose(1, 0, 2, 3).reshape(leaf_target.shape[0], columns, width)
    correction = jnp.einsum("kij,kci->kjc", leaf_link, parent_t, preferred_element_type=jnp.float32)
    leaf_w = (leaf_solved.astype(jnp.float32) - correction).astype(jnp.bfloat16)
    leaf_result = apply_transposed(leaf_inverse, leaf_w).astype(jnp.bfloat16)
    return (leaf_result, node_result, middle_result, top_result)


def solution(mesh):
    cores = len({d.core_on_chip for d in mesh.devices[:, 0]})
    y_size = len({d.coords[1] for d in mesh.devices[0]})
    grid = mesh.devices.reshape(mesh.shape["row"] // cores, cores, -1, y_size)
    view = Mesh(grid, ("x", "core", "z", "y"))
    placed = (
        P((*ROW, *COL), None, None),
        P((*ROW, *COL), None, None),
        P((*ROW, *COL), None, None),
        P((*ROW, *COL)),
        P((*ROW, *COL), None, None),
        P((*ROW, *COL), None, None),
        P((*ROW, *COL), None, None),
        P(ROW),
        P(ROW, None, None),
        P(ROW, None, None),
        P(ROW, None, None),
        P(ROW),
        P(),
        P(),
    )
    return jax.shard_map(
        local,
        mesh=view,
        in_specs=placed,
        out_specs=(
            P((*ROW, *COL), None, None),
            P((*ROW, *COL), None, None),
            P(ROW, None, None),
            P(),
        ),
        check_vma=False,
    )
```

```python
import jax
import jax.numpy as jnp
from jax import lax
from jax.experimental import pallas as pl
from jax.experimental.pallas import tpu as pltpu
from jax.sharding import Mesh
from jax.sharding import PartitionSpec as P

ROW = ("x", "core")
COL = ("z", "y")


def apply_block(matrix, vectors):
    return jnp.einsum("nij,njr->nir", matrix, vectors, preferred_element_type=jnp.float32)


def apply_transposed(matrix, vectors):
    return jnp.einsum("nij,nir->njr", matrix, vectors, preferred_element_type=jnp.float32)


def piece_block(matrix, pieces):
    return jnp.einsum("nij,ncj->nci", matrix, pieces, preferred_element_type=jnp.float32)


def piece_transposed(matrix, pieces):
    return jnp.einsum("nij,nci->ncj", matrix, pieces, preferred_element_type=jnp.float32)


def slot_sums(targets, count, values):
    slots = lax.iota(jnp.int32, count)
    select = (slots[:, None] == targets[None, :]).astype(jnp.float32)
    return jnp.einsum("sk,k...->s...", select, values, precision=lax.Precision.HIGHEST)


def split_slot_sums(targets, count, values):
    slots = lax.iota(jnp.int32, count)
    select = (slots[:, None] == targets[None, :]).astype(jnp.bfloat16)
    high = values.astype(jnp.bfloat16)
    low = (values - high.astype(jnp.float32)).astype(jnp.bfloat16)
    total = jnp.einsum("sk,k...->s...", select, high, preferred_element_type=jnp.float32)
    return total + jnp.einsum("sk,k...->s...", select, low, preferred_element_type=jnp.float32)


def leaf_backward_kernel(parent_ref, pieces_ref, solved_ref, link_t_ref, inverse_t_ref, out_ref):
    pieces = pieces_ref[...]
    parent_t = pieces.reshape(pieces.shape[0] * pieces.shape[1], pieces.shape[2])
    correction = lax.dot_general(
        link_t_ref[...], parent_t, (((1,), (1,)), ((), ())), preferred_element_type=jnp.float32
    )
    w = (solved_ref[...].astype(jnp.float32) - correction).astype(jnp.bfloat16)
    out_ref[...] = jnp.dot(inverse_t_ref[...], w, preferred_element_type=jnp.float32).astype(out_ref.dtype)


def leaf_backward(targets, gathered, leaf_solved, leaf_link, leaf_inverse):
    count, width, columns = leaf_solved.shape
    peers, _, chunk, _ = gathered.shape
    link_t = leaf_link.transpose(0, 2, 1)
    inverse_t = leaf_inverse.transpose(0, 2, 1)

    def own(k, parent):
        return (k, 0, 0)

    def parent_pieces(k, parent):
        return (0, parent[k], 0, 0)

    grid_spec = pltpu.PrefetchScalarGridSpec(
        num_scalar_prefetch=1,
        grid=(count,),
        in_specs=[
            pl.BlockSpec((peers, None, chunk, width), parent_pieces),
            pl.BlockSpec((None, width, columns), own),
            pl.BlockSpec((None, width, width), own),
            pl.BlockSpec((None, width, width), own),
        ],
        out_specs=pl.BlockSpec((None, width, columns), own),
    )
    cost = pl.CostEstimate(
        flops=4 * count * width * width * columns,
        transcendentals=0,
        bytes_accessed=2 * count * (3 * width * columns + 2 * width * width),
    )
    return pl.pallas_call(
        leaf_backward_kernel,
        grid_spec=grid_spec,
        out_shape=jax.ShapeDtypeStruct(leaf_solved.shape, jnp.bfloat16),
        cost_estimate=cost,
    )(targets, gathered, leaf_solved, link_t, inverse_t)


def local(
    leaf_rhs,
    leaf_inverse,
    leaf_link,
    leaf_parent,
    node_rhs,
    node_inverse,
    node_link,
    node_parent,
    middle_rhs,
    middle_inverse,
    middle_link,
    middle_parent,
    top_rhs,
    top_inverse,
):
    y_size = lax.axis_size("y")
    z_size = lax.axis_size("z")
    peers = y_size * z_size
    col_index = lax.axis_index(COL)
    width = leaf_rhs.shape[1]
    columns = leaf_rhs.shape[2]
    chunk = columns // peers
    middle_count = middle_rhs.shape[0]
    top_count = top_rhs.shape[0]
    leaf_target = leaf_parent % peers
    middle_target = node_parent % middle_count
    start = col_index * chunk

    node_mats = lax.all_gather(jnp.concatenate([node_inverse, node_link], axis=0), COL, axis=0, tiled=False)
    row_inverse = node_mats[:, 0]
    row_link = node_mats[:, 1]

    leaf_solved = apply_block(leaf_inverse, leaf_rhs).astype(jnp.bfloat16)
    leaf_update = jnp.einsum("kij,kjr->kri", leaf_link, leaf_solved, preferred_element_type=jnp.float32)
    half = peers // 2
    y_index = lax.axis_index("y")
    rhs_t = node_rhs.transpose(0, 2, 1)
    sums = []
    for group in range(2):
        targets = leaf_target - group * half
        entries = split_slot_sums(targets, half, leaf_update).astype(jnp.bfloat16)
        if group == 1:
            entries = jnp.concatenate([entries, rhs_t], axis=0)
        count = entries.shape[0]
        entries = entries.reshape(count, z_size, y_size, chunk, width).transpose(2, 1, 0, 3, 4)
        arrivals = [lax.dynamic_index_in_dim(entries, y_index, 0, keepdims=False)]
        for shift in range(1, y_size):
            outbound = lax.dynamic_index_in_dim(entries, (y_index + shift) % y_size, 0, keepdims=False)
            pairs = [(i, (i + shift) % y_size) for i in range(y_size)]
            arrivals.append(lax.ppermute(outbound, "y", pairs))
        partial = sum(a[:, :half].astype(jnp.float32) for a in arrivals).astype(jnp.bfloat16)
        if group == 1:
            partial = jnp.concatenate([partial, jnp.stack([a[:, half] for a in arrivals], axis=1)], axis=1)
        incoming = lax.all_to_all(partial, "z", 0, 0, tiled=True)
        sums.append(jnp.sum(incoming[:, :half].astype(jnp.float32), axis=0))
    node_sum = jnp.concatenate(sums, axis=0)
    offsets = (y_index - lax.iota(jnp.int32, y_size)) % y_size
    own_rhs = jnp.take(incoming[:, half:], offsets, axis=1).reshape(peers, chunk, width)
    node_y = (own_rhs.astype(jnp.float32) - node_sum).astype(jnp.bfloat16)
    node_solved = piece_block(row_inverse, node_y).astype(jnp.bfloat16)
    middle_sum = slot_sums(middle_target, middle_count, piece_block(row_link, node_solved))
    middle_piece = lax.dynamic_slice_in_dim(middle_rhs, start, chunk, 2).transpose(0, 2, 1)
    middle_y = (middle_piece.astype(jnp.float32) - middle_sum).astype(jnp.bfloat16)
    middle_solved = piece_block(middle_inverse, middle_y).astype(jnp.bfloat16)
    top_term = slot_sums(middle_parent, top_count, piece_block(middle_link, middle_solved))
    top_sum = top_term
    rows = lax.axis_size(ROW)
    step = 1
    while step < rows:
        top_sum = top_sum + lax.ppermute(top_sum, ROW, [(i, i ^ step) for i in range(rows)])
        step *= 2
    top_piece = lax.dynamic_slice_in_dim(top_rhs, start, chunk, 2).transpose(0, 2, 1)
    top_y = (top_piece.astype(jnp.float32) - top_sum).astype(jnp.bfloat16)
    top_solved = piece_block(top_inverse, top_y).astype(jnp.bfloat16)
    top_part = piece_transposed(top_inverse, top_solved).astype(jnp.bfloat16)
    middle_w = (
        middle_solved.astype(jnp.float32) - piece_transposed(middle_link, top_part[middle_parent])
    ).astype(jnp.bfloat16)
    middle_part = piece_transposed(middle_inverse, middle_w).astype(jnp.bfloat16)
    node_w = (
        node_solved.astype(jnp.float32) - piece_transposed(row_link, middle_part[middle_target])
    ).astype(jnp.bfloat16)
    node_part = piece_transposed(row_inverse, node_w).astype(jnp.bfloat16)

    parts = jnp.concatenate([node_part, middle_part, top_part], axis=0)
    gathered = lax.all_gather(lax.all_gather(parts, "y", axis=0, tiled=False), "z", axis=0, tiled=True)
    upper = gathered[:, peers:].transpose(1, 3, 0, 2).reshape(middle_count + top_count, width, columns)
    middle_result = upper[:middle_count]
    top_result = upper[middle_count:]
    node_result = lax.dynamic_index_in_dim(gathered, col_index, 1).transpose(1, 3, 0, 2).reshape(1, width, columns)

    leaf_result = leaf_backward(leaf_target, gathered, leaf_solved, leaf_link, leaf_inverse)
    return (leaf_result, node_result, middle_result, top_result)


def solution(mesh):
    cores = len({d.core_on_chip for d in mesh.devices[:, 0]})
    y_size = len({d.coords[1] for d in mesh.devices[0]})
    grid = mesh.devices.reshape(mesh.shape["row"] // cores, cores, -1, y_size)
    view = Mesh(grid, ("x", "core", "z", "y"))
    placed = (
        P((*ROW, *COL), None, None),
        P((*ROW, *COL), None, None),
        P((*ROW, *COL), None, None),
        P((*ROW, *COL)),
        P((*ROW, *COL), None, None),
        P((*ROW, *COL), None, None),
        P((*ROW, *COL), None, None),
        P(ROW),
        P(ROW, None, None),
        P(ROW, None, None),
        P(ROW, None, None),
        P(ROW),
        P(),
        P(),
    )
    return jax.shard_map(
        local,
        mesh=view,
        in_specs=placed,
        out_specs=(
            P((*ROW, *COL), None, None),
            P((*ROW, *COL), None, None),
            P(ROW, None, None),
            P(),
        ),
        check_vma=False,
    )
```

```python
import jax
import jax.numpy as jnp
from jax import lax
from jax.sharding import Mesh
from jax.sharding import PartitionSpec as P

ROW = ("x", "core")
COL = ("z", "y")


def apply_block(matrix, vectors):
    return jnp.einsum("nij,njr->nir", matrix, vectors, preferred_element_type=jnp.float32)


def apply_transposed(matrix, vectors):
    return jnp.einsum("nij,nir->njr", matrix, vectors, preferred_element_type=jnp.float32)


def piece_block(matrix, pieces):
    return jnp.einsum("nij,ncj->nci", matrix, pieces, preferred_element_type=jnp.float32)


def piece_transposed(matrix, pieces):
    return jnp.einsum("nij,nci->ncj", matrix, pieces, preferred_element_type=jnp.float32)


def slot_sums(targets, count, values):
    slots = lax.iota(jnp.int32, count)
    select = (slots[:, None] == targets[None, :]).astype(jnp.float32)
    return jnp.einsum("sk,k...->s...", select, values, precision=lax.Precision.HIGHEST)


def split_slot_sums(targets, count, values):
    slots = lax.iota(jnp.int32, count)
    select = (slots[:, None] == targets[None, :]).astype(jnp.bfloat16)
    high = values.astype(jnp.bfloat16)
    low = (values - high.astype(jnp.float32)).astype(jnp.bfloat16)
    total = jnp.einsum("sk,k...->s...", select, high, preferred_element_type=jnp.float32)
    return total + jnp.einsum("sk,k...->s...", select, low, preferred_element_type=jnp.float32)


def local(
    leaf_rhs,
    leaf_inverse,
    leaf_link,
    leaf_parent,
    node_rhs,
    node_inverse,
    node_link,
    node_parent,
    middle_rhs,
    middle_inverse,
    middle_link,
    middle_parent,
    top_rhs,
    top_inverse,
):
    y_size = lax.axis_size("y")
    z_size = lax.axis_size("z")
    peers = y_size * z_size
    col_index = lax.axis_index(COL)
    width = leaf_rhs.shape[1]
    columns = leaf_rhs.shape[2]
    chunk = columns // peers
    middle_count = middle_rhs.shape[0]
    top_count = top_rhs.shape[0]
    leaf_target = leaf_parent % peers
    middle_target = node_parent % middle_count
    start = col_index * chunk

    node_mats = lax.all_gather(jnp.concatenate([node_inverse, node_link], axis=0), COL, axis=0, tiled=False)
    row_inverse = node_mats[:, 0]
    row_link = node_mats[:, 1]

    leaf_solved = apply_block(leaf_inverse, leaf_rhs).astype(jnp.bfloat16)
    leaf_update = jnp.einsum("kij,kjr->kri", leaf_link, leaf_solved, preferred_element_type=jnp.float32)
    half = peers // 2
    y_index = lax.axis_index("y")
    rhs_t = node_rhs.transpose(0, 2, 1)
    sums = []
    for group in range(2):
        targets = leaf_target - group * half
        entries = split_slot_sums(targets, half, leaf_update).astype(jnp.bfloat16)
        if group == 1:
            entries = jnp.concatenate([entries, rhs_t], axis=0)
        count = entries.shape[0]
        entries = entries.reshape(count, z_size, y_size, chunk, width).transpose(2, 1, 0, 3, 4)
        arrivals = [lax.dynamic_index_in_dim(entries, y_index, 0, keepdims=False)]
        for shift in range(1, y_size):
            outbound = lax.dynamic_index_in_dim(entries, (y_index + shift) % y_size, 0, keepdims=False)
            pairs = [(i, (i + shift) % y_size) for i in range(y_size)]
            arrivals.append(lax.ppermute(outbound, "y", pairs))
        partial = sum(a[:, :half].astype(jnp.float32) for a in arrivals).astype(jnp.bfloat16)
        if group == 1:
            partial = jnp.concatenate([partial, jnp.stack([a[:, half] for a in arrivals], axis=1)], axis=1)
        incoming = lax.all_to_all(partial, "z", 0, 0, tiled=True)
        sums.append(jnp.sum(incoming[:, :half].astype(jnp.float32), axis=0))
    node_sum = jnp.concatenate(sums, axis=0)
    offsets = (y_index - lax.iota(jnp.int32, y_size)) % y_size
    own_rhs = jnp.take(incoming[:, half:], offsets, axis=1).reshape(peers, chunk, width)
    node_y = (own_rhs.astype(jnp.float32) - node_sum).astype(jnp.bfloat16)
    node_solved = piece_block(row_inverse, node_y).astype(jnp.bfloat16)
    middle_sum = slot_sums(middle_target, middle_count, piece_block(row_link, node_solved))
    middle_piece = lax.dynamic_slice_in_dim(middle_rhs, start, chunk, 2).transpose(0, 2, 1)
    middle_y = (middle_piece.astype(jnp.float32) - middle_sum).astype(jnp.bfloat16)
    middle_solved = piece_block(middle_inverse, middle_y).astype(jnp.bfloat16)
    top_term = slot_sums(middle_parent, top_count, piece_block(middle_link, middle_solved))
    top_sum = top_term
    rows = lax.axis_size(ROW)
    step = 1
    while step < rows:
        top_sum = top_sum + lax.ppermute(top_sum, ROW, [(i, i ^ step) for i in range(rows)])
        step *= 2
    top_piece = lax.dynamic_slice_in_dim(top_rhs, start, chunk, 2).transpose(0, 2, 1)
    top_y = (top_piece.astype(jnp.float32) - top_sum).astype(jnp.bfloat16)
    top_solved = piece_block(top_inverse, top_y).astype(jnp.bfloat16)
    top_part = piece_transposed(top_inverse, top_solved).astype(jnp.bfloat16)
    middle_w = (
        middle_solved.astype(jnp.float32) - piece_transposed(middle_link, top_part[middle_parent])
    ).astype(jnp.bfloat16)
    middle_part = piece_transposed(middle_inverse, middle_w).astype(jnp.bfloat16)
    node_w = (
        node_solved.astype(jnp.float32) - piece_transposed(row_link, middle_part[middle_target])
    ).astype(jnp.bfloat16)
    node_part = piece_transposed(row_inverse, node_w).astype(jnp.bfloat16)

    parts = jnp.concatenate([node_part, middle_part, top_part], axis=0)
    arrivals = [parts]
    for shift in range(1, y_size):
        pairs = [(i, (i + shift) % y_size) for i in range(y_size)]
        arrivals.append(lax.ppermute(parts, "y", pairs))
    by_y = jnp.take(jnp.stack(arrivals), (y_index - lax.iota(jnp.int32, y_size)) % y_size, axis=0)
    gathered = lax.all_gather(by_y, "z", axis=0, tiled=True)
    upper = gathered[:, peers:].transpose(1, 3, 0, 2).reshape(middle_count + top_count, width, columns)
    middle_result = upper[:middle_count]
    top_result = upper[middle_count:]
    node_result = lax.dynamic_index_in_dim(gathered, col_index, 1).transpose(1, 3, 0, 2).reshape(1, width, columns)

    parent_t = gathered[:, leaf_target].transpose(1, 0, 2, 3).reshape(leaf_target.shape[0], columns, width)
    correction = jnp.einsum("kij,kci->kjc", leaf_link, parent_t, preferred_element_type=jnp.float32)
    leaf_w = (leaf_solved.astype(jnp.float32) - correction).astype(jnp.bfloat16)
    leaf_result = apply_transposed(leaf_inverse, leaf_w).astype(jnp.bfloat16)
    return (leaf_result, node_result, middle_result, top_result)


def solution(mesh):
    cores = len({d.core_on_chip for d in mesh.devices[:, 0]})
    y_size = len({d.coords[1] for d in mesh.devices[0]})
    grid = mesh.devices.reshape(mesh.shape["row"] // cores, cores, -1, y_size)
    view = Mesh(grid, ("x", "core", "z", "y"))
    placed = (
        P((*ROW, *COL), None, None),
        P((*ROW, *COL), None, None),
        P((*ROW, *COL), None, None),
        P((*ROW, *COL)),
        P((*ROW, *COL), None, None),
        P((*ROW, *COL), None, None),
        P((*ROW, *COL), None, None),
        P(ROW),
        P(ROW, None, None),
        P(ROW, None, None),
        P(ROW, None, None),
        P(ROW),
        P(),
        P(),
    )
    return jax.shard_map(
        local,
        mesh=view,
        in_specs=placed,
        out_specs=(
            P((*ROW, *COL), None, None),
            P((*ROW, *COL), None, None),
            P(ROW, None, None),
            P(),
        ),
        check_vma=False,
    )
```

```python
import jax
import jax.numpy as jnp
from jax import lax
from jax.sharding import Mesh
from jax.sharding import PartitionSpec as P

ROW = ("x", "core")
COL = ("z", "y")


def apply_block(matrix, vectors):
    return jnp.einsum("nij,njr->nir", matrix, vectors, preferred_element_type=jnp.float32)


def apply_transposed(matrix, vectors):
    return jnp.einsum("nij,nir->njr", matrix, vectors, preferred_element_type=jnp.float32)


def piece_block(matrix, pieces):
    return jnp.einsum("nij,ncj->nci", matrix, pieces, preferred_element_type=jnp.float32)


def piece_transposed(matrix, pieces):
    return jnp.einsum("nij,nci->ncj", matrix, pieces, preferred_element_type=jnp.float32)


def slot_sums(targets, count, values):
    slots = lax.iota(jnp.int32, count)
    select = (slots[:, None] == targets[None, :]).astype(jnp.float32)
    return jnp.einsum("sk,k...->s...", select, values, precision=lax.Precision.HIGHEST)


def split_slot_sums(targets, count, values):
    slots = lax.iota(jnp.int32, count)
    select = (slots[:, None] == targets[None, :]).astype(jnp.bfloat16)
    high = values.astype(jnp.bfloat16)
    low = (values - high.astype(jnp.float32)).astype(jnp.bfloat16)
    total = jnp.einsum("sk,k...->s...", select, high, preferred_element_type=jnp.float32)
    return total + jnp.einsum("sk,k...->s...", select, low, preferred_element_type=jnp.float32)


def local(
    leaf_rhs,
    leaf_inverse,
    leaf_link,
    leaf_parent,
    node_rhs,
    node_inverse,
    node_link,
    node_parent,
    middle_rhs,
    middle_inverse,
    middle_link,
    middle_parent,
    top_rhs,
    top_inverse,
):
    y_size = lax.axis_size("y")
    z_size = lax.axis_size("z")
    peers = y_size * z_size
    col_index = lax.axis_index(COL)
    width = leaf_rhs.shape[1]
    columns = leaf_rhs.shape[2]
    chunk = columns // peers
    middle_count = middle_rhs.shape[0]
    top_count = top_rhs.shape[0]
    leaf_target = leaf_parent % peers
    middle_target = node_parent % middle_count
    start = col_index * chunk

    y_index = lax.axis_index("y")
    own_mats = jnp.concatenate([node_inverse, node_link], axis=0)
    mats = [own_mats]
    for shift in range(1, y_size):
        pairs = [(i, (i + shift) % y_size) for i in range(y_size)]
        mats.append(lax.ppermute(own_mats, "y", pairs))
    mats_by_y = jnp.take(jnp.stack(mats), (y_index - lax.iota(jnp.int32, y_size)) % y_size, axis=0)
    node_mats = lax.all_gather(mats_by_y, "z", axis=0, tiled=True)
    row_inverse = node_mats[:, 0]
    row_link = node_mats[:, 1]

    leaf_solved = apply_block(leaf_inverse, leaf_rhs).astype(jnp.bfloat16)
    leaf_update = jnp.einsum("kij,kjr->kri", leaf_link, leaf_solved, preferred_element_type=jnp.float32)
    half = peers // 2
    rhs_t = node_rhs.transpose(0, 2, 1)
    sums = []
    for group in range(2):
        targets = leaf_target - group * half
        entries = split_slot_sums(targets, half, leaf_update).astype(jnp.bfloat16)
        if group == 1:
            entries = jnp.concatenate([entries, rhs_t], axis=0)
        count = entries.shape[0]
        entries = entries.reshape(count, z_size, y_size, chunk, width).transpose(2, 1, 0, 3, 4)
        arrivals = [lax.dynamic_index_in_dim(entries, y_index, 0, keepdims=False)]
        for shift in range(1, y_size):
            outbound = lax.dynamic_index_in_dim(entries, (y_index + shift) % y_size, 0, keepdims=False)
            pairs = [(i, (i + shift) % y_size) for i in range(y_size)]
            arrivals.append(lax.ppermute(outbound, "y", pairs))
        partial = sum(a[:, :half].astype(jnp.float32) for a in arrivals).astype(jnp.bfloat16)
        if group == 1:
            partial = jnp.concatenate([partial, jnp.stack([a[:, half] for a in arrivals], axis=1)], axis=1)
        incoming = lax.all_to_all(partial, "z", 0, 0, tiled=True)
        sums.append(jnp.sum(incoming[:, :half].astype(jnp.float32), axis=0))
    node_sum = jnp.concatenate(sums, axis=0)
    offsets = (y_index - lax.iota(jnp.int32, y_size)) % y_size
    own_rhs = jnp.take(incoming[:, half:], offsets, axis=1).reshape(peers, chunk, width)
    node_y = (own_rhs.astype(jnp.float32) - node_sum).astype(jnp.bfloat16)
    node_solved = piece_block(row_inverse, node_y).astype(jnp.bfloat16)
    middle_sum = slot_sums(middle_target, middle_count, piece_block(row_link, node_solved))
    middle_piece = lax.dynamic_slice_in_dim(middle_rhs, start, chunk, 2).transpose(0, 2, 1)
    middle_y = (middle_piece.astype(jnp.float32) - middle_sum).astype(jnp.bfloat16)
    middle_solved = piece_block(middle_inverse, middle_y).astype(jnp.bfloat16)
    top_term = slot_sums(middle_parent, top_count, piece_block(middle_link, middle_solved))
    top_sum = top_term
    rows = lax.axis_size(ROW)
    step = 1
    while step < rows:
        top_sum = top_sum + lax.ppermute(top_sum, ROW, [(i, i ^ step) for i in range(rows)])
        step *= 2
    top_piece = lax.dynamic_slice_in_dim(top_rhs, start, chunk, 2).transpose(0, 2, 1)
    top_y = (top_piece.astype(jnp.float32) - top_sum).astype(jnp.bfloat16)
    top_solved = piece_block(top_inverse, top_y).astype(jnp.bfloat16)
    top_part = piece_transposed(top_inverse, top_solved).astype(jnp.bfloat16)
    middle_w = (
        middle_solved.astype(jnp.float32) - piece_transposed(middle_link, top_part[middle_parent])
    ).astype(jnp.bfloat16)
    middle_part = piece_transposed(middle_inverse, middle_w).astype(jnp.bfloat16)
    node_w = (
        node_solved.astype(jnp.float32) - piece_transposed(row_link, middle_part[middle_target])
    ).astype(jnp.bfloat16)
    node_part = piece_transposed(row_inverse, node_w).astype(jnp.bfloat16)

    parts = jnp.concatenate([node_part, middle_part, top_part], axis=0)
    arrivals = [parts]
    for shift in range(1, y_size):
        pairs = [(i, (i + shift) % y_size) for i in range(y_size)]
        arrivals.append(lax.ppermute(parts, "y", pairs))
    by_y = jnp.take(jnp.stack(arrivals), (y_index - lax.iota(jnp.int32, y_size)) % y_size, axis=0)
    gathered = lax.all_gather(by_y, "z", axis=0, tiled=True)
    upper = gathered[:, peers:].transpose(1, 3, 0, 2).reshape(middle_count + top_count, width, columns)
    middle_result = upper[:middle_count]
    top_result = upper[middle_count:]
    node_result = lax.dynamic_index_in_dim(gathered, col_index, 1).transpose(1, 3, 0, 2).reshape(1, width, columns)

    parent_t = gathered[:, leaf_target].transpose(1, 0, 2, 3).reshape(leaf_target.shape[0], columns, width)
    correction = jnp.einsum("kij,kci->kjc", leaf_link, parent_t, preferred_element_type=jnp.float32)
    leaf_w = (leaf_solved.astype(jnp.float32) - correction).astype(jnp.bfloat16)
    leaf_result = apply_transposed(leaf_inverse, leaf_w).astype(jnp.bfloat16)
    return (leaf_result, node_result, middle_result, top_result)


def solution(mesh):
    cores = len({d.core_on_chip for d in mesh.devices[:, 0]})
    y_size = len({d.coords[1] for d in mesh.devices[0]})
    grid = mesh.devices.reshape(mesh.shape["row"] // cores, cores, -1, y_size)
    view = Mesh(grid, ("x", "core", "z", "y"))
    placed = (
        P((*ROW, *COL), None, None),
        P((*ROW, *COL), None, None),
        P((*ROW, *COL), None, None),
        P((*ROW, *COL)),
        P((*ROW, *COL), None, None),
        P((*ROW, *COL), None, None),
        P((*ROW, *COL), None, None),
        P(ROW),
        P(ROW, None, None),
        P(ROW, None, None),
        P(ROW, None, None),
        P(ROW),
        P(),
        P(),
    )
    return jax.shard_map(
        local,
        mesh=view,
        in_specs=placed,
        out_specs=(
            P((*ROW, *COL), None, None),
            P((*ROW, *COL), None, None),
            P(ROW, None, None),
            P(),
        ),
        check_vma=False,
    )
```

```python
import jax
import jax.numpy as jnp
from jax import lax
from jax.experimental import pallas as pl
from jax.sharding import Mesh
from jax.sharding import PartitionSpec as P

ROW = ("x", "core")
COL = ("z", "y")


def apply_block(matrix, vectors):
    return jnp.einsum("nij,njr->nir", matrix, vectors, preferred_element_type=jnp.float32)


def apply_transposed(matrix, vectors):
    return jnp.einsum("nij,nir->njr", matrix, vectors, preferred_element_type=jnp.float32)


def piece_block(matrix, pieces):
    return jnp.einsum("nij,ncj->nci", matrix, pieces, preferred_element_type=jnp.float32)


def piece_transposed(matrix, pieces):
    return jnp.einsum("nij,nci->ncj", matrix, pieces, preferred_element_type=jnp.float32)


def slot_sums(targets, count, values):
    slots = lax.iota(jnp.int32, count)
    select = (slots[:, None] == targets[None, :]).astype(jnp.float32)
    return jnp.einsum("sk,k...->s...", select, values, precision=lax.Precision.HIGHEST)


def split_slot_sums(targets, count, values):
    slots = lax.iota(jnp.int32, count)
    select = (slots[:, None] == targets[None, :]).astype(jnp.bfloat16)
    high = values.astype(jnp.bfloat16)
    low = (values - high.astype(jnp.float32)).astype(jnp.bfloat16)
    total = jnp.einsum("sk,k...->s...", select, high, preferred_element_type=jnp.float32)
    return total + jnp.einsum("sk,k...->s...", select, low, preferred_element_type=jnp.float32)


def leaf_backward_kernel(parent_ref, solved_ref, link_t_ref, inverse_t_ref, out_ref):
    for k in range(parent_ref.shape[0]):
        pieces = parent_ref[k]
        parent_t = pieces.reshape(pieces.shape[0] * pieces.shape[1], pieces.shape[2])
        correction = lax.dot_general(
            link_t_ref[k], parent_t, (((1,), (1,)), ((), ())), preferred_element_type=jnp.float32
        )
        w = (solved_ref[k].astype(jnp.float32) - correction).astype(jnp.bfloat16)
        out_ref[k] = jnp.dot(inverse_t_ref[k], w, preferred_element_type=jnp.float32).astype(out_ref.dtype)


def leaf_backward(parents, leaf_solved, leaf_link, leaf_inverse):
    count, width, columns = leaf_solved.shape
    per_step = max(d for d in range(1, 5) if count % d == 0)
    pieces = parents.shape[1:]

    def own(step):
        return (step, 0, 0)

    cost = pl.CostEstimate(
        flops=4 * count * width * width * columns,
        transcendentals=0,
        bytes_accessed=2 * count * (3 * width * columns + 2 * width * width),
    )
    return pl.pallas_call(
        leaf_backward_kernel,
        grid=(count // per_step,),
        in_specs=[
            pl.BlockSpec((per_step, *pieces), lambda step: (step, 0, 0, 0)),
            pl.BlockSpec((per_step, width, columns), own),
            pl.BlockSpec((per_step, width, width), own),
            pl.BlockSpec((per_step, width, width), own),
        ],
        out_specs=pl.BlockSpec((per_step, width, columns), own),
        out_shape=jax.ShapeDtypeStruct(leaf_solved.shape, jnp.bfloat16),
        cost_estimate=cost,
    )(parents, leaf_solved, leaf_link.transpose(0, 2, 1), leaf_inverse.transpose(0, 2, 1))


def local(
    leaf_rhs,
    leaf_inverse,
    leaf_link,
    leaf_parent,
    node_rhs,
    node_inverse,
    node_link,
    node_parent,
    middle_rhs,
    middle_inverse,
    middle_link,
    middle_parent,
    top_rhs,
    top_inverse,
):
    y_size = lax.axis_size("y")
    z_size = lax.axis_size("z")
    peers = y_size * z_size
    col_index = lax.axis_index(COL)
    width = leaf_rhs.shape[1]
    columns = leaf_rhs.shape[2]
    chunk = columns // peers
    middle_count = middle_rhs.shape[0]
    top_count = top_rhs.shape[0]
    leaf_target = leaf_parent % peers
    middle_target = node_parent % middle_count
    start = col_index * chunk

    y_index = lax.axis_index("y")
    own_mats = jnp.concatenate([node_inverse, node_link], axis=0)
    mats = [own_mats]
    for shift in range(1, y_size):
        pairs = [(i, (i + shift) % y_size) for i in range(y_size)]
        mats.append(lax.ppermute(own_mats, "y", pairs))
    mats_by_y = jnp.take(jnp.stack(mats), (y_index - lax.iota(jnp.int32, y_size)) % y_size, axis=0)
    node_mats = lax.all_gather(mats_by_y, "z", axis=0, tiled=True)
    row_inverse = node_mats[:, 0]
    row_link = node_mats[:, 1]

    leaf_solved = apply_block(leaf_inverse, leaf_rhs).astype(jnp.bfloat16)
    leaf_update = jnp.einsum("kij,kjr->kri", leaf_link, leaf_solved, preferred_element_type=jnp.float32)
    half = peers // 2
    rhs_t = node_rhs.transpose(0, 2, 1)
    sums = []
    for group in range(2):
        targets = leaf_target - group * half
        entries = split_slot_sums(targets, half, leaf_update).astype(jnp.bfloat16)
        if group == 1:
            entries = jnp.concatenate([entries, rhs_t], axis=0)
        count = entries.shape[0]
        entries = entries.reshape(count, z_size, y_size, chunk, width).transpose(2, 1, 0, 3, 4)
        arrivals = [lax.dynamic_index_in_dim(entries, y_index, 0, keepdims=False)]
        for shift in range(1, y_size):
            outbound = lax.dynamic_index_in_dim(entries, (y_index + shift) % y_size, 0, keepdims=False)
            pairs = [(i, (i + shift) % y_size) for i in range(y_size)]
            arrivals.append(lax.ppermute(outbound, "y", pairs))
        partial = sum(a[:, :half].astype(jnp.float32) for a in arrivals).astype(jnp.bfloat16)
        if group == 1:
            partial = jnp.concatenate([partial, jnp.stack([a[:, half] for a in arrivals], axis=1)], axis=1)
        incoming = lax.all_to_all(partial, "z", 0, 0, tiled=True)
        sums.append(jnp.sum(incoming[:, :half].astype(jnp.float32), axis=0))
    node_sum = jnp.concatenate(sums, axis=0)
    offsets = (y_index - lax.iota(jnp.int32, y_size)) % y_size
    own_rhs = jnp.take(incoming[:, half:], offsets, axis=1).reshape(peers, chunk, width)
    node_y = (own_rhs.astype(jnp.float32) - node_sum).astype(jnp.bfloat16)
    node_solved = piece_block(row_inverse, node_y).astype(jnp.bfloat16)
    middle_sum = slot_sums(middle_target, middle_count, piece_block(row_link, node_solved))
    middle_piece = lax.dynamic_slice_in_dim(middle_rhs, start, chunk, 2).transpose(0, 2, 1)
    middle_y = (middle_piece.astype(jnp.float32) - middle_sum).astype(jnp.bfloat16)
    middle_solved = piece_block(middle_inverse, middle_y).astype(jnp.bfloat16)
    top_term = slot_sums(middle_parent, top_count, piece_block(middle_link, middle_solved))
    top_sum = top_term
    rows = lax.axis_size(ROW)
    step = 1
    while step < rows:
        top_sum = top_sum + lax.ppermute(top_sum, ROW, [(i, i ^ step) for i in range(rows)])
        step *= 2
    top_piece = lax.dynamic_slice_in_dim(top_rhs, start, chunk, 2).transpose(0, 2, 1)
    top_y = (top_piece.astype(jnp.float32) - top_sum).astype(jnp.bfloat16)
    top_solved = piece_block(top_inverse, top_y).astype(jnp.bfloat16)
    top_part = piece_transposed(top_inverse, top_solved).astype(jnp.bfloat16)
    middle_w = (
        middle_solved.astype(jnp.float32) - piece_transposed(middle_link, top_part[middle_parent])
    ).astype(jnp.bfloat16)
    middle_part = piece_transposed(middle_inverse, middle_w).astype(jnp.bfloat16)
    node_w = (
        node_solved.astype(jnp.float32) - piece_transposed(row_link, middle_part[middle_target])
    ).astype(jnp.bfloat16)
    node_part = piece_transposed(row_inverse, node_w).astype(jnp.bfloat16)

    parts = jnp.concatenate([node_part, middle_part, top_part], axis=0)
    arrivals = [parts]
    for shift in range(1, y_size):
        pairs = [(i, (i + shift) % y_size) for i in range(y_size)]
        arrivals.append(lax.ppermute(parts, "y", pairs))
    by_y = jnp.take(jnp.stack(arrivals), (y_index - lax.iota(jnp.int32, y_size)) % y_size, axis=0)
    gathered = lax.all_gather(by_y, "z", axis=0, tiled=True)
    upper = gathered[:, peers:].transpose(1, 3, 0, 2).reshape(middle_count + top_count, width, columns)
    middle_result = upper[:middle_count]
    top_result = upper[middle_count:]
    node_result = lax.dynamic_index_in_dim(gathered, col_index, 1).transpose(1, 3, 0, 2).reshape(1, width, columns)

    parents = gathered[:, leaf_target].transpose(1, 0, 2, 3)
    leaf_result = leaf_backward(parents, leaf_solved, leaf_link, leaf_inverse)
    return (leaf_result, node_result, middle_result, top_result)


def solution(mesh):
    cores = len({d.core_on_chip for d in mesh.devices[:, 0]})
    y_size = len({d.coords[1] for d in mesh.devices[0]})
    grid = mesh.devices.reshape(mesh.shape["row"] // cores, cores, -1, y_size)
    view = Mesh(grid, ("x", "core", "z", "y"))
    placed = (
        P((*ROW, *COL), None, None),
        P((*ROW, *COL), None, None),
        P((*ROW, *COL), None, None),
        P((*ROW, *COL)),
        P((*ROW, *COL), None, None),
        P((*ROW, *COL), None, None),
        P((*ROW, *COL), None, None),
        P(ROW),
        P(ROW, None, None),
        P(ROW, None, None),
        P(ROW, None, None),
        P(ROW),
        P(),
        P(),
    )
    return jax.shard_map(
        local,
        mesh=view,
        in_specs=placed,
        out_specs=(
            P((*ROW, *COL), None, None),
            P((*ROW, *COL), None, None),
            P(ROW, None, None),
            P(),
        ),
        check_vma=False,
    )
```

```python
import jax
import jax.numpy as jnp
from jax import lax
from jax.experimental import pallas as pl
from jax.sharding import Mesh
from jax.sharding import PartitionSpec as P

ROW = ("x", "core")
COL = ("z", "y")


def apply_block(matrix, vectors):
    return jnp.einsum("nij,njr->nir", matrix, vectors, preferred_element_type=jnp.float32)


def apply_transposed(matrix, vectors):
    return jnp.einsum("nij,nir->njr", matrix, vectors, preferred_element_type=jnp.float32)


def piece_block(matrix, pieces):
    return jnp.einsum("nij,ncj->nci", matrix, pieces, preferred_element_type=jnp.float32)


def piece_transposed(matrix, pieces):
    return jnp.einsum("nij,nci->ncj", matrix, pieces, preferred_element_type=jnp.float32)


def slot_sums(targets, count, values):
    slots = lax.iota(jnp.int32, count)
    select = (slots[:, None] == targets[None, :]).astype(jnp.float32)
    return jnp.einsum("sk,k...->s...", select, values, precision=lax.Precision.HIGHEST)


def split_slot_sums(targets, count, values):
    slots = lax.iota(jnp.int32, count)
    select = (slots[:, None] == targets[None, :]).astype(jnp.bfloat16)
    high = values.astype(jnp.bfloat16)
    low = (values - high.astype(jnp.float32)).astype(jnp.bfloat16)
    total = jnp.einsum("sk,k...->s...", select, high, preferred_element_type=jnp.float32)
    return total + jnp.einsum("sk,k...->s...", select, low, preferred_element_type=jnp.float32)


def leaf_backward_kernel(parent_ref, solved_ref, link_t_ref, inverse_t_ref, out_ref):
    def one_leaf(k, carry):
        pieces = parent_ref[k]
        parent_t = pieces.reshape(pieces.shape[0] * pieces.shape[1], pieces.shape[2])
        correction = lax.dot_general(
            link_t_ref[k], parent_t, (((1,), (1,)), ((), ())), preferred_element_type=jnp.float32
        )
        w = (solved_ref[k].astype(jnp.float32) - correction).astype(jnp.bfloat16)
        out_ref[k] = jnp.dot(inverse_t_ref[k], w, preferred_element_type=jnp.float32).astype(out_ref.dtype)
        return carry

    lax.fori_loop(0, parent_ref.shape[0], one_leaf, 0)


def leaf_backward(parents, leaf_solved, leaf_link, leaf_inverse):
    count, width, columns = leaf_solved.shape
    per_step = max(d for d in range(1, 5) if count % d == 0)
    pieces = parents.shape[1:]

    def own(step):
        return (step, 0, 0)

    cost = pl.CostEstimate(
        flops=4 * count * width * width * columns,
        transcendentals=0,
        bytes_accessed=2 * count * (3 * width * columns + 2 * width * width),
    )
    return pl.pallas_call(
        leaf_backward_kernel,
        grid=(count // per_step,),
        in_specs=[
            pl.BlockSpec((per_step, *pieces), lambda step: (step, 0, 0, 0)),
            pl.BlockSpec((per_step, width, columns), own),
            pl.BlockSpec((per_step, width, width), own),
            pl.BlockSpec((per_step, width, width), own),
        ],
        out_specs=pl.BlockSpec((per_step, width, columns), own),
        out_shape=jax.ShapeDtypeStruct(leaf_solved.shape, jnp.bfloat16),
        cost_estimate=cost,
    )(parents, leaf_solved, leaf_link.transpose(0, 2, 1), leaf_inverse.transpose(0, 2, 1))


def local(
    leaf_rhs,
    leaf_inverse,
    leaf_link,
    leaf_parent,
    node_rhs,
    node_inverse,
    node_link,
    node_parent,
    middle_rhs,
    middle_inverse,
    middle_link,
    middle_parent,
    top_rhs,
    top_inverse,
):
    y_size = lax.axis_size("y")
    z_size = lax.axis_size("z")
    peers = y_size * z_size
    col_index = lax.axis_index(COL)
    width = leaf_rhs.shape[1]
    columns = leaf_rhs.shape[2]
    chunk = columns // peers
    middle_count = middle_rhs.shape[0]
    top_count = top_rhs.shape[0]
    leaf_target = leaf_parent % peers
    middle_target = node_parent % middle_count
    start = col_index * chunk

    y_index = lax.axis_index("y")
    own_mats = jnp.concatenate([node_inverse, node_link], axis=0)
    mats = [own_mats]
    for shift in range(1, y_size):
        pairs = [(i, (i + shift) % y_size) for i in range(y_size)]
        mats.append(lax.ppermute(own_mats, "y", pairs))
    mats_by_y = jnp.take(jnp.stack(mats), (y_index - lax.iota(jnp.int32, y_size)) % y_size, axis=0)
    node_mats = lax.all_gather(mats_by_y, "z", axis=0, tiled=True)
    row_inverse = node_mats[:, 0]
    row_link = node_mats[:, 1]

    leaf_solved = apply_block(leaf_inverse, leaf_rhs).astype(jnp.bfloat16)
    leaf_update = jnp.einsum("kij,kjr->kri", leaf_link, leaf_solved, preferred_element_type=jnp.float32)
    half = peers // 2
    rhs_t = node_rhs.transpose(0, 2, 1)
    sums = []
    for group in range(2):
        targets = leaf_target - group * half
        entries = split_slot_sums(targets, half, leaf_update).astype(jnp.bfloat16)
        if group == 1:
            entries = jnp.concatenate([entries, rhs_t], axis=0)
        count = entries.shape[0]
        entries = entries.reshape(count, z_size, y_size, chunk, width).transpose(2, 1, 0, 3, 4)
        arrivals = [lax.dynamic_index_in_dim(entries, y_index, 0, keepdims=False)]
        for shift in range(1, y_size):
            outbound = lax.dynamic_index_in_dim(entries, (y_index + shift) % y_size, 0, keepdims=False)
            pairs = [(i, (i + shift) % y_size) for i in range(y_size)]
            arrivals.append(lax.ppermute(outbound, "y", pairs))
        partial = sum(a[:, :half].astype(jnp.float32) for a in arrivals).astype(jnp.bfloat16)
        if group == 1:
            partial = jnp.concatenate([partial, jnp.stack([a[:, half] for a in arrivals], axis=1)], axis=1)
        incoming = lax.all_to_all(partial, "z", 0, 0, tiled=True)
        sums.append(jnp.sum(incoming[:, :half].astype(jnp.float32), axis=0))
    node_sum = jnp.concatenate(sums, axis=0)
    offsets = (y_index - lax.iota(jnp.int32, y_size)) % y_size
    own_rhs = jnp.take(incoming[:, half:], offsets, axis=1).reshape(peers, chunk, width)
    node_y = (own_rhs.astype(jnp.float32) - node_sum).astype(jnp.bfloat16)
    node_solved = piece_block(row_inverse, node_y).astype(jnp.bfloat16)
    middle_sum = slot_sums(middle_target, middle_count, piece_block(row_link, node_solved))
    middle_piece = lax.dynamic_slice_in_dim(middle_rhs, start, chunk, 2).transpose(0, 2, 1)
    middle_y = (middle_piece.astype(jnp.float32) - middle_sum).astype(jnp.bfloat16)
    middle_solved = piece_block(middle_inverse, middle_y).astype(jnp.bfloat16)
    top_term = slot_sums(middle_parent, top_count, piece_block(middle_link, middle_solved))
    top_sum = top_term
    rows = lax.axis_size(ROW)
    step = 1
    while step < rows:
        top_sum = top_sum + lax.ppermute(top_sum, ROW, [(i, i ^ step) for i in range(rows)])
        step *= 2
    top_piece = lax.dynamic_slice_in_dim(top_rhs, start, chunk, 2).transpose(0, 2, 1)
    top_y = (top_piece.astype(jnp.float32) - top_sum).astype(jnp.bfloat16)
    top_solved = piece_block(top_inverse, top_y).astype(jnp.bfloat16)
    top_part = piece_transposed(top_inverse, top_solved).astype(jnp.bfloat16)
    middle_w = (
        middle_solved.astype(jnp.float32) - piece_transposed(middle_link, top_part[middle_parent])
    ).astype(jnp.bfloat16)
    middle_part = piece_transposed(middle_inverse, middle_w).astype(jnp.bfloat16)
    node_w = (
        node_solved.astype(jnp.float32) - piece_transposed(row_link, middle_part[middle_target])
    ).astype(jnp.bfloat16)
    node_part = piece_transposed(row_inverse, node_w).astype(jnp.bfloat16)

    parts = jnp.concatenate([node_part, middle_part, top_part], axis=0)
    arrivals = [parts]
    for shift in range(1, y_size):
        pairs = [(i, (i + shift) % y_size) for i in range(y_size)]
        arrivals.append(lax.ppermute(parts, "y", pairs))
    by_y = jnp.take(jnp.stack(arrivals), (y_index - lax.iota(jnp.int32, y_size)) % y_size, axis=0)
    gathered = lax.all_gather(by_y, "z", axis=0, tiled=True)
    upper = gathered[:, peers:].transpose(1, 3, 0, 2).reshape(middle_count + top_count, width, columns)
    middle_result = upper[:middle_count]
    top_result = upper[middle_count:]
    node_result = lax.dynamic_index_in_dim(gathered, col_index, 1).transpose(1, 3, 0, 2).reshape(1, width, columns)

    parents = gathered[:, leaf_target].transpose(1, 0, 2, 3)
    leaf_result = leaf_backward(parents, leaf_solved, leaf_link, leaf_inverse)
    return (leaf_result, node_result, middle_result, top_result)


def solution(mesh):
    cores = len({d.core_on_chip for d in mesh.devices[:, 0]})
    y_size = len({d.coords[1] for d in mesh.devices[0]})
    grid = mesh.devices.reshape(mesh.shape["row"] // cores, cores, -1, y_size)
    view = Mesh(grid, ("x", "core", "z", "y"))
    placed = (
        P((*ROW, *COL), None, None),
        P((*ROW, *COL), None, None),
        P((*ROW, *COL), None, None),
        P((*ROW, *COL)),
        P((*ROW, *COL), None, None),
        P((*ROW, *COL), None, None),
        P((*ROW, *COL), None, None),
        P(ROW),
        P(ROW, None, None),
        P(ROW, None, None),
        P(ROW, None, None),
        P(ROW),
        P(),
        P(),
    )
    return jax.shard_map(
        local,
        mesh=view,
        in_specs=placed,
        out_specs=(
            P((*ROW, *COL), None, None),
            P((*ROW, *COL), None, None),
            P(ROW, None, None),
            P(),
        ),
        check_vma=False,
    )
```

```python
import jax
import jax.numpy as jnp
from jax import lax
from jax.experimental import pallas as pl
from jax.sharding import Mesh
from jax.sharding import PartitionSpec as P

ROW = ("x", "core")
COL = ("z", "y")


def apply_block(matrix, vectors):
    return jnp.einsum("nij,njr->nir", matrix, vectors, preferred_element_type=jnp.float32)


def apply_transposed(matrix, vectors):
    return jnp.einsum("nij,nir->njr", matrix, vectors, preferred_element_type=jnp.float32)


def piece_block(matrix, pieces):
    return jnp.einsum("nij,ncj->nci", matrix, pieces, preferred_element_type=jnp.float32)


def piece_transposed(matrix, pieces):
    return jnp.einsum("nij,nci->ncj", matrix, pieces, preferred_element_type=jnp.float32)


def slot_sums(targets, count, values):
    slots = lax.iota(jnp.int32, count)
    select = (slots[:, None] == targets[None, :]).astype(jnp.float32)
    return jnp.einsum("sk,k...->s...", select, values, precision=lax.Precision.HIGHEST)


def split_slot_sums(targets, count, values):
    slots = lax.iota(jnp.int32, count)
    select = (slots[:, None] == targets[None, :]).astype(jnp.bfloat16)
    high = values.astype(jnp.bfloat16)
    low = (values - high.astype(jnp.float32)).astype(jnp.bfloat16)
    total = jnp.einsum("sk,k...->s...", select, high, preferred_element_type=jnp.float32)
    return total + jnp.einsum("sk,k...->s...", select, low, preferred_element_type=jnp.float32)


def leaf_backward_kernel(parent_ref, solved_ref, link_t_ref, inverse_t_ref, out_ref):
    for k in range(parent_ref.shape[0]):
        pieces = parent_ref[k]
        parent_t = pieces.reshape(pieces.shape[0] * pieces.shape[1], pieces.shape[2])
        correction = lax.dot_general(
            link_t_ref[k], parent_t, (((1,), (1,)), ((), ())), preferred_element_type=jnp.float32
        )
        w = (solved_ref[k].astype(jnp.float32) - correction).astype(jnp.bfloat16)
        out_ref[k] = jnp.dot(inverse_t_ref[k], w, preferred_element_type=jnp.float32).astype(out_ref.dtype)


def leaf_backward(parents, leaf_solved, leaf_link, leaf_inverse):
    count, width, columns = leaf_solved.shape
    per_step = max(d for d in range(1, 5) if count % d == 0)
    pieces = parents.shape[1:]

    def own(step):
        return (step, 0, 0)

    cost = pl.CostEstimate(
        flops=4 * count * width * width * columns,
        transcendentals=0,
        bytes_accessed=2 * count * (3 * width * columns + 2 * width * width),
    )
    return pl.pallas_call(
        leaf_backward_kernel,
        grid=(count // per_step,),
        in_specs=[
            pl.BlockSpec((per_step, *pieces), lambda step: (step, 0, 0, 0)),
            pl.BlockSpec((per_step, width, columns), own),
            pl.BlockSpec((per_step, width, width), own),
            pl.BlockSpec((per_step, width, width), own),
        ],
        out_specs=pl.BlockSpec((per_step, width, columns), own),
        out_shape=jax.ShapeDtypeStruct(leaf_solved.shape, jnp.bfloat16),
        cost_estimate=cost,
    )(parents, leaf_solved, leaf_link.transpose(0, 2, 1), leaf_inverse.transpose(0, 2, 1))


def local(
    leaf_rhs,
    leaf_inverse,
    leaf_link,
    leaf_parent,
    node_rhs,
    node_inverse,
    node_link,
    node_parent,
    middle_rhs,
    middle_inverse,
    middle_link,
    middle_parent,
    top_rhs,
    top_inverse,
):
    y_size = lax.axis_size("y")
    z_size = lax.axis_size("z")
    peers = y_size * z_size
    col_index = lax.axis_index(COL)
    width = leaf_rhs.shape[1]
    columns = leaf_rhs.shape[2]
    chunk = columns // peers
    middle_count = middle_rhs.shape[0]
    top_count = top_rhs.shape[0]
    leaf_target = leaf_parent % peers
    middle_target = node_parent % middle_count
    start = col_index * chunk

    y_index = lax.axis_index("y")
    own_mats = jnp.concatenate([node_inverse, node_link], axis=0)
    mats = [own_mats]
    for shift in range(1, y_size):
        pairs = [(i, (i + shift) % y_size) for i in range(y_size)]
        mats.append(lax.ppermute(own_mats, "y", pairs))
    mats_by_y = jnp.take(jnp.stack(mats), (y_index - lax.iota(jnp.int32, y_size)) % y_size, axis=0)
    node_mats = lax.all_gather(mats_by_y, "z", axis=0, tiled=True)
    row_inverse = node_mats[:, 0]
    row_link = node_mats[:, 1]

    leaf_solved = apply_block(leaf_inverse, leaf_rhs).astype(jnp.bfloat16)
    leaf_update = jnp.einsum("kij,kjr->kri", leaf_link, leaf_solved, preferred_element_type=jnp.float32)
    half = peers // 2
    rhs_t = node_rhs.transpose(0, 2, 1)
    sums = []
    for group in range(2):
        targets = leaf_target - group * half
        entries = split_slot_sums(targets, half, leaf_update).astype(jnp.bfloat16)
        if group == 1:
            entries = jnp.concatenate([entries, rhs_t], axis=0)
        count = entries.shape[0]
        entries = entries.reshape(count, z_size, y_size, chunk, width).transpose(2, 1, 0, 3, 4)
        arrivals = [lax.dynamic_index_in_dim(entries, y_index, 0, keepdims=False)]
        for shift in range(1, y_size):
            outbound = lax.dynamic_index_in_dim(entries, (y_index + shift) % y_size, 0, keepdims=False)
            pairs = [(i, (i + shift) % y_size) for i in range(y_size)]
            arrivals.append(lax.ppermute(outbound, "y", pairs))
        partial = sum(a[:, :half].astype(jnp.float32) for a in arrivals).astype(jnp.bfloat16)
        if group == 1:
            partial = jnp.concatenate([partial, jnp.stack([a[:, half] for a in arrivals], axis=1)], axis=1)
        incoming = lax.all_to_all(partial, "z", 0, 0, tiled=True)
        sums.append(jnp.sum(incoming[:, :half].astype(jnp.float32), axis=0))
    node_sum = jnp.concatenate(sums, axis=0)
    offsets = (y_index - lax.iota(jnp.int32, y_size)) % y_size
    own_rhs = jnp.take(incoming[:, half:], offsets, axis=1).reshape(peers, chunk, width)
    node_y = (own_rhs.astype(jnp.float32) - node_sum).astype(jnp.bfloat16)
    node_solved = piece_block(row_inverse, node_y).astype(jnp.bfloat16)
    middle_sum = slot_sums(middle_target, middle_count, piece_block(row_link, node_solved))
    middle_piece = lax.dynamic_slice_in_dim(middle_rhs, start, chunk, 2).transpose(0, 2, 1)
    middle_y = (middle_piece.astype(jnp.float32) - middle_sum).astype(jnp.bfloat16)
    middle_solved = piece_block(middle_inverse, middle_y).astype(jnp.bfloat16)
    top_term = slot_sums(middle_parent, top_count, piece_block(middle_link, middle_solved))
    rows = lax.axis_size(ROW)
    terms = [top_term]
    for shift in range(1, rows):
        terms.append(lax.ppermute(top_term, ROW, [(i, (i + shift) % rows) for i in range(rows)]))
    in_row_order = jnp.take(jnp.stack(terms), (lax.axis_index(ROW) - lax.iota(jnp.int32, rows)) % rows, axis=0)
    top_sum = jnp.sum(in_row_order, axis=0)
    top_piece = lax.dynamic_slice_in_dim(top_rhs, start, chunk, 2).transpose(0, 2, 1)
    top_y = (top_piece.astype(jnp.float32) - top_sum).astype(jnp.bfloat16)
    top_solved = piece_block(top_inverse, top_y).astype(jnp.bfloat16)
    top_part = piece_transposed(top_inverse, top_solved).astype(jnp.bfloat16)
    middle_w = (
        middle_solved.astype(jnp.float32) - piece_transposed(middle_link, top_part[middle_parent])
    ).astype(jnp.bfloat16)
    middle_part = piece_transposed(middle_inverse, middle_w).astype(jnp.bfloat16)
    node_w = (
        node_solved.astype(jnp.float32) - piece_transposed(row_link, middle_part[middle_target])
    ).astype(jnp.bfloat16)
    node_part = piece_transposed(row_inverse, node_w).astype(jnp.bfloat16)

    parts = jnp.concatenate([node_part, middle_part, top_part], axis=0)
    arrivals = [parts]
    for shift in range(1, y_size):
        pairs = [(i, (i + shift) % y_size) for i in range(y_size)]
        arrivals.append(lax.ppermute(parts, "y", pairs))
    by_y = jnp.take(jnp.stack(arrivals), (y_index - lax.iota(jnp.int32, y_size)) % y_size, axis=0)
    gathered = lax.all_gather(by_y, "z", axis=0, tiled=True)
    upper = gathered[:, peers:].transpose(1, 3, 0, 2).reshape(middle_count + top_count, width, columns)
    middle_result = upper[:middle_count]
    top_result = upper[middle_count:]
    node_result = lax.dynamic_index_in_dim(gathered, col_index, 1).transpose(1, 3, 0, 2).reshape(1, width, columns)

    parents = gathered[:, leaf_target].transpose(1, 0, 2, 3)
    leaf_result = leaf_backward(parents, leaf_solved, leaf_link, leaf_inverse)
    return (leaf_result, node_result, middle_result, top_result)


def solution(mesh):
    cores = len({d.core_on_chip for d in mesh.devices[:, 0]})
    y_size = len({d.coords[1] for d in mesh.devices[0]})
    grid = mesh.devices.reshape(mesh.shape["row"] // cores, cores, -1, y_size)
    view = Mesh(grid, ("x", "core", "z", "y"))
    placed = (
        P((*ROW, *COL), None, None),
        P((*ROW, *COL), None, None),
        P((*ROW, *COL), None, None),
        P((*ROW, *COL)),
        P((*ROW, *COL), None, None),
        P((*ROW, *COL), None, None),
        P((*ROW, *COL), None, None),
        P(ROW),
        P(ROW, None, None),
        P(ROW, None, None),
        P(ROW, None, None),
        P(ROW),
        P(),
        P(),
    )
    return jax.shard_map(
        local,
        mesh=view,
        in_specs=placed,
        out_specs=(
            P((*ROW, *COL), None, None),
            P((*ROW, *COL), None, None),
            P(ROW, None, None),
            P(),
        ),
        check_vma=False,
    )
```

```python
import jax
import jax.numpy as jnp
from jax import lax
from jax.experimental import pallas as pl
from jax.sharding import Mesh
from jax.sharding import PartitionSpec as P

ROW = ("x", "core")
COL = ("z", "y")


def apply_block(matrix, vectors):
    return jnp.einsum("nij,njr->nir", matrix, vectors, preferred_element_type=jnp.float32)


def apply_transposed(matrix, vectors):
    return jnp.einsum("nij,nir->njr", matrix, vectors, preferred_element_type=jnp.float32)


def piece_block(matrix, pieces):
    return jnp.einsum("nij,ncj->nci", matrix, pieces, preferred_element_type=jnp.float32)


def piece_transposed(matrix, pieces):
    return jnp.einsum("nij,nci->ncj", matrix, pieces, preferred_element_type=jnp.float32)


def slot_sums(targets, count, values):
    slots = lax.iota(jnp.int32, count)
    select = (slots[:, None] == targets[None, :]).astype(jnp.float32)
    return jnp.einsum("sk,k...->s...", select, values, precision=lax.Precision.HIGHEST)


def split_slot_sums(targets, count, values):
    slots = lax.iota(jnp.int32, count)
    select = (slots[:, None] == targets[None, :]).astype(jnp.bfloat16)
    high = values.astype(jnp.bfloat16)
    low = (values - high.astype(jnp.float32)).astype(jnp.bfloat16)
    total = jnp.einsum("sk,k...->s...", select, high, preferred_element_type=jnp.float32)
    return total + jnp.einsum("sk,k...->s...", select, low, preferred_element_type=jnp.float32)


def leaf_backward_kernel(parent_ref, solved_ref, link_t_ref, inverse_t_ref, out_ref):
    for k in range(parent_ref.shape[0]):
        pieces = parent_ref[k]
        parent_t = pieces.reshape(pieces.shape[0] * pieces.shape[1], pieces.shape[2])
        correction = lax.dot_general(
            link_t_ref[k], parent_t, (((1,), (1,)), ((), ())), preferred_element_type=jnp.float32
        )
        w = (solved_ref[k].astype(jnp.float32) - correction).astype(jnp.bfloat16)
        out_ref[k] = jnp.dot(inverse_t_ref[k], w, preferred_element_type=jnp.float32).astype(out_ref.dtype)


def leaf_backward(parents, leaf_solved, leaf_link, leaf_inverse):
    count, width, columns = leaf_solved.shape
    per_step = max(d for d in range(1, 9) if count % d == 0)
    pieces = parents.shape[1:]

    def own(step):
        return (step, 0, 0)

    cost = pl.CostEstimate(
        flops=4 * count * width * width * columns,
        transcendentals=0,
        bytes_accessed=2 * count * (3 * width * columns + 2 * width * width),
    )
    return pl.pallas_call(
        leaf_backward_kernel,
        grid=(count // per_step,),
        in_specs=[
            pl.BlockSpec((per_step, *pieces), lambda step: (step, 0, 0, 0)),
            pl.BlockSpec((per_step, width, columns), own),
            pl.BlockSpec((per_step, width, width), own),
            pl.BlockSpec((per_step, width, width), own),
        ],
        out_specs=pl.BlockSpec((per_step, width, columns), own),
        out_shape=jax.ShapeDtypeStruct(leaf_solved.shape, jnp.bfloat16),
        cost_estimate=cost,
    )(parents, leaf_solved, leaf_link.transpose(0, 2, 1), leaf_inverse.transpose(0, 2, 1))


def local(
    leaf_rhs,
    leaf_inverse,
    leaf_link,
    leaf_parent,
    node_rhs,
    node_inverse,
    node_link,
    node_parent,
    middle_rhs,
    middle_inverse,
    middle_link,
    middle_parent,
    top_rhs,
    top_inverse,
):
    y_size = lax.axis_size("y")
    z_size = lax.axis_size("z")
    peers = y_size * z_size
    col_index = lax.axis_index(COL)
    width = leaf_rhs.shape[1]
    columns = leaf_rhs.shape[2]
    chunk = columns // peers
    middle_count = middle_rhs.shape[0]
    top_count = top_rhs.shape[0]
    leaf_target = leaf_parent % peers
    middle_target = node_parent % middle_count
    start = col_index * chunk

    y_index = lax.axis_index("y")
    own_mats = jnp.concatenate([node_inverse, node_link], axis=0)
    mats = [own_mats]
    for shift in range(1, y_size):
        pairs = [(i, (i + shift) % y_size) for i in range(y_size)]
        mats.append(lax.ppermute(own_mats, "y", pairs))
    mats_by_y = jnp.take(jnp.stack(mats), (y_index - lax.iota(jnp.int32, y_size)) % y_size, axis=0)
    node_mats = lax.all_gather(mats_by_y, "z", axis=0, tiled=True)
    row_inverse = node_mats[:, 0]
    row_link = node_mats[:, 1]

    leaf_solved = apply_block(leaf_inverse, leaf_rhs).astype(jnp.bfloat16)
    leaf_update = jnp.einsum("kij,kjr->kri", leaf_link, leaf_solved, preferred_element_type=jnp.float32)
    half = peers // 2
    rhs_t = node_rhs.transpose(0, 2, 1)
    sums = []
    for group in range(2):
        targets = leaf_target - group * half
        entries = split_slot_sums(targets, half, leaf_update).astype(jnp.bfloat16)
        if group == 1:
            entries = jnp.concatenate([entries, rhs_t], axis=0)
        count = entries.shape[0]
        entries = entries.reshape(count, z_size, y_size, chunk, width).transpose(2, 1, 0, 3, 4)
        arrivals = [lax.dynamic_index_in_dim(entries, y_index, 0, keepdims=False)]
        for shift in range(1, y_size):
            outbound = lax.dynamic_index_in_dim(entries, (y_index + shift) % y_size, 0, keepdims=False)
            pairs = [(i, (i + shift) % y_size) for i in range(y_size)]
            arrivals.append(lax.ppermute(outbound, "y", pairs))
        partial = sum(a[:, :half].astype(jnp.float32) for a in arrivals).astype(jnp.bfloat16)
        if group == 1:
            partial = jnp.concatenate([partial, jnp.stack([a[:, half] for a in arrivals], axis=1)], axis=1)
        incoming = lax.all_to_all(partial, "z", 0, 0, tiled=True)
        sums.append(jnp.sum(incoming[:, :half].astype(jnp.float32), axis=0))
    node_sum = jnp.concatenate(sums, axis=0)
    offsets = (y_index - lax.iota(jnp.int32, y_size)) % y_size
    own_rhs = jnp.take(incoming[:, half:], offsets, axis=1).reshape(peers, chunk, width)
    node_y = (own_rhs.astype(jnp.float32) - node_sum).astype(jnp.bfloat16)
    node_solved = piece_block(row_inverse, node_y).astype(jnp.bfloat16)
    middle_sum = slot_sums(middle_target, middle_count, piece_block(row_link, node_solved))
    middle_piece = lax.dynamic_slice_in_dim(middle_rhs, start, chunk, 2).transpose(0, 2, 1)
    middle_y = (middle_piece.astype(jnp.float32) - middle_sum).astype(jnp.bfloat16)
    middle_solved = piece_block(middle_inverse, middle_y).astype(jnp.bfloat16)
    top_term = slot_sums(middle_parent, top_count, piece_block(middle_link, middle_solved))
    top_sum = top_term
    rows = lax.axis_size(ROW)
    step = 1
    while step < rows:
        top_sum = top_sum + lax.ppermute(top_sum, ROW, [(i, i ^ step) for i in range(rows)])
        step *= 2
    top_piece = lax.dynamic_slice_in_dim(top_rhs, start, chunk, 2).transpose(0, 2, 1)
    top_y = (top_piece.astype(jnp.float32) - top_sum).astype(jnp.bfloat16)
    top_solved = piece_block(top_inverse, top_y).astype(jnp.bfloat16)
    top_part = piece_transposed(top_inverse, top_solved).astype(jnp.bfloat16)
    middle_w = (
        middle_solved.astype(jnp.float32) - piece_transposed(middle_link, top_part[middle_parent])
    ).astype(jnp.bfloat16)
    middle_part = piece_transposed(middle_inverse, middle_w).astype(jnp.bfloat16)
    node_w = (
        node_solved.astype(jnp.float32) - piece_transposed(row_link, middle_part[middle_target])
    ).astype(jnp.bfloat16)
    node_part = piece_transposed(row_inverse, node_w).astype(jnp.bfloat16)

    parts = jnp.concatenate([node_part, middle_part, top_part], axis=0)
    arrivals = [parts]
    for shift in range(1, y_size):
        pairs = [(i, (i + shift) % y_size) for i in range(y_size)]
        arrivals.append(lax.ppermute(parts, "y", pairs))
    by_y = jnp.take(jnp.stack(arrivals), (y_index - lax.iota(jnp.int32, y_size)) % y_size, axis=0)
    gathered = lax.all_gather(by_y, "z", axis=0, tiled=True)
    upper = gathered[:, peers:].transpose(1, 3, 0, 2).reshape(middle_count + top_count, width, columns)
    middle_result = upper[:middle_count]
    top_result = upper[middle_count:]
    node_result = lax.dynamic_index_in_dim(gathered, col_index, 1).transpose(1, 3, 0, 2).reshape(1, width, columns)

    parents = gathered[:, leaf_target].transpose(1, 0, 2, 3)
    leaf_result = leaf_backward(parents, leaf_solved, leaf_link, leaf_inverse)
    return (leaf_result, node_result, middle_result, top_result)


def solution(mesh):
    cores = len({d.core_on_chip for d in mesh.devices[:, 0]})
    y_size = len({d.coords[1] for d in mesh.devices[0]})
    grid = mesh.devices.reshape(mesh.shape["row"] // cores, cores, -1, y_size)
    view = Mesh(grid, ("x", "core", "z", "y"))
    placed = (
        P((*ROW, *COL), None, None),
        P((*ROW, *COL), None, None),
        P((*ROW, *COL), None, None),
        P((*ROW, *COL)),
        P((*ROW, *COL), None, None),
        P((*ROW, *COL), None, None),
        P((*ROW, *COL), None, None),
        P(ROW),
        P(ROW, None, None),
        P(ROW, None, None),
        P(ROW, None, None),
        P(ROW),
        P(),
        P(),
    )
    return jax.shard_map(
        local,
        mesh=view,
        in_specs=placed,
        out_specs=(
            P((*ROW, *COL), None, None),
            P((*ROW, *COL), None, None),
            P(ROW, None, None),
            P(),
        ),
        check_vma=False,
    )
```

```python
import jax
import jax.numpy as jnp
from jax import lax
from jax.experimental import pallas as pl
from jax.sharding import Mesh
from jax.sharding import PartitionSpec as P

ROW = ("x", "core")
COL = ("z", "y")


def apply_block(matrix, vectors):
    return jnp.einsum("nij,njr->nir", matrix, vectors, preferred_element_type=jnp.float32)


def apply_transposed(matrix, vectors):
    return jnp.einsum("nij,nir->njr", matrix, vectors, preferred_element_type=jnp.float32)


def piece_block(matrix, pieces):
    return jnp.einsum("nij,ncj->nci", matrix, pieces, preferred_element_type=jnp.float32)


def piece_transposed(matrix, pieces):
    return jnp.einsum("nij,nci->ncj", matrix, pieces, preferred_element_type=jnp.float32)


def slot_sums(targets, count, values):
    slots = lax.iota(jnp.int32, count)
    select = (slots[:, None] == targets[None, :]).astype(jnp.float32)
    return jnp.einsum("sk,k...->s...", select, values, precision=lax.Precision.HIGHEST)


def split_slot_sums(targets, count, values):
    slots = lax.iota(jnp.int32, count)
    select = (slots[:, None] == targets[None, :]).astype(jnp.bfloat16)
    high = values.astype(jnp.bfloat16)
    low = (values - high.astype(jnp.float32)).astype(jnp.bfloat16)
    total = jnp.einsum("sk,k...->s...", select, high, preferred_element_type=jnp.float32)
    return total + jnp.einsum("sk,k...->s...", select, low, preferred_element_type=jnp.float32)


def leaf_backward_kernel(parent_ref, solved_ref, link_t_ref, inverse_t_ref, out_ref):
    for k in range(parent_ref.shape[0]):
        pieces = parent_ref[k]
        parent_t = pieces.reshape(pieces.shape[0] * pieces.shape[1], pieces.shape[2])
        correction = lax.dot_general(
            link_t_ref[k], parent_t, (((1,), (1,)), ((), ())), preferred_element_type=jnp.float32
        )
        w = (solved_ref[k].astype(jnp.float32) - correction).astype(jnp.bfloat16)
        out_ref[k] = jnp.dot(inverse_t_ref[k], w, preferred_element_type=jnp.float32).astype(out_ref.dtype)


def leaf_backward(parents, leaf_solved, leaf_link, leaf_inverse):
    count, width, columns = leaf_solved.shape
    per_step = max(d for d in range(1, 9) if count % d == 0)
    pieces = parents.shape[1:]

    def own(step):
        return (step, 0, 0)

    cost = pl.CostEstimate(
        flops=4 * count * width * width * columns,
        transcendentals=0,
        bytes_accessed=2 * count * (3 * width * columns + 2 * width * width),
    )
    return pl.pallas_call(
        leaf_backward_kernel,
        grid=(count // per_step,),
        in_specs=[
            pl.BlockSpec((per_step, *pieces), lambda step: (step, 0, 0, 0)),
            pl.BlockSpec((per_step, width, columns), own),
            pl.BlockSpec((per_step, width, width), own),
            pl.BlockSpec((per_step, width, width), own),
        ],
        out_specs=pl.BlockSpec((per_step, width, columns), own),
        out_shape=jax.ShapeDtypeStruct(leaf_solved.shape, jnp.bfloat16),
        cost_estimate=cost,
    )(parents, leaf_solved, leaf_link.transpose(0, 2, 1), leaf_inverse.transpose(0, 2, 1))


def local(
    leaf_rhs,
    leaf_inverse,
    leaf_link,
    leaf_parent,
    node_rhs,
    node_inverse,
    node_link,
    node_parent,
    middle_rhs,
    middle_inverse,
    middle_link,
    middle_parent,
    top_rhs,
    top_inverse,
):
    y_size = lax.axis_size("y")
    z_size = lax.axis_size("z")
    peers = y_size * z_size
    col_index = lax.axis_index(COL)
    width = leaf_rhs.shape[1]
    columns = leaf_rhs.shape[2]
    chunk = columns // peers
    middle_count = middle_rhs.shape[0]
    top_count = top_rhs.shape[0]
    leaf_target = leaf_parent % peers
    middle_target = node_parent % middle_count
    start = col_index * chunk

    y_index = lax.axis_index("y")
    own_mats = jnp.concatenate([node_inverse, node_link], axis=0)
    mats = [own_mats]
    for shift in range(1, y_size):
        pairs = [(i, (i + shift) % y_size) for i in range(y_size)]
        mats.append(lax.ppermute(own_mats, "y", pairs))
    mats_by_y = jnp.take(jnp.stack(mats), (y_index - lax.iota(jnp.int32, y_size)) % y_size, axis=0)
    node_mats = lax.all_gather(mats_by_y, "z", axis=0, tiled=True)
    row_inverse = node_mats[:, 0]
    row_link = node_mats[:, 1]

    leaf_solved = apply_block(leaf_inverse, leaf_rhs).astype(jnp.bfloat16)
    leaf_update = jnp.einsum("kij,kjr->kri", leaf_link, leaf_solved, preferred_element_type=jnp.float32)
    half = peers // 2
    rhs_t = node_rhs.transpose(0, 2, 1)
    sums = []
    for group in range(2):
        targets = leaf_target - group * half
        entries = split_slot_sums(targets, half, leaf_update).astype(jnp.bfloat16)
        if group == 1:
            entries = jnp.concatenate([entries, rhs_t], axis=0)
        count = entries.shape[0]
        entries = entries.reshape(count, z_size, y_size, chunk, width).transpose(2, 1, 0, 3, 4)
        arrivals = [lax.dynamic_index_in_dim(entries, y_index, 0, keepdims=False)]
        for shift in range(1, y_size):
            outbound = lax.dynamic_index_in_dim(entries, (y_index + shift) % y_size, 0, keepdims=False)
            pairs = [(i, (i + shift) % y_size) for i in range(y_size)]
            arrivals.append(lax.ppermute(outbound, "y", pairs))
        partial = sum(a[:, :half].astype(jnp.float32) for a in arrivals).astype(jnp.bfloat16)
        if group == 1:
            partial = jnp.concatenate([partial, jnp.stack([a[:, half] for a in arrivals], axis=1)], axis=1)
        incoming = lax.all_to_all(partial, "z", 0, 0, tiled=True)
        sums.append(jnp.sum(incoming[:, :half].astype(jnp.float32), axis=0))
    node_sum = jnp.concatenate(sums, axis=0)
    offsets = (y_index - lax.iota(jnp.int32, y_size)) % y_size
    own_rhs = jnp.take(incoming[:, half:], offsets, axis=1).reshape(peers, chunk, width)
    node_y = (own_rhs.astype(jnp.float32) - node_sum).astype(jnp.bfloat16)
    node_solved = piece_block(row_inverse, node_y).astype(jnp.bfloat16)
    middle_sum = split_slot_sums(middle_target, middle_count, piece_block(row_link, node_solved))
    middle_piece = lax.dynamic_slice_in_dim(middle_rhs, start, chunk, 2).transpose(0, 2, 1)
    middle_y = (middle_piece.astype(jnp.float32) - middle_sum).astype(jnp.bfloat16)
    middle_solved = piece_block(middle_inverse, middle_y).astype(jnp.bfloat16)
    top_term = split_slot_sums(middle_parent, top_count, piece_block(middle_link, middle_solved))
    top_sum = top_term
    rows = lax.axis_size(ROW)
    step = 1
    while step < rows:
        top_sum = top_sum + lax.ppermute(top_sum, ROW, [(i, i ^ step) for i in range(rows)])
        step *= 2
    top_piece = lax.dynamic_slice_in_dim(top_rhs, start, chunk, 2).transpose(0, 2, 1)
    top_y = (top_piece.astype(jnp.float32) - top_sum).astype(jnp.bfloat16)
    top_solved = piece_block(top_inverse, top_y).astype(jnp.bfloat16)
    top_part = piece_transposed(top_inverse, top_solved).astype(jnp.bfloat16)
    middle_w = (
        middle_solved.astype(jnp.float32) - piece_transposed(middle_link, top_part[middle_parent])
    ).astype(jnp.bfloat16)
    middle_part = piece_transposed(middle_inverse, middle_w).astype(jnp.bfloat16)
    node_w = (
        node_solved.astype(jnp.float32) - piece_transposed(row_link, middle_part[middle_target])
    ).astype(jnp.bfloat16)
    node_part = piece_transposed(row_inverse, node_w).astype(jnp.bfloat16)

    parts = jnp.concatenate([node_part, middle_part, top_part], axis=0)
    arrivals = [parts]
    for shift in range(1, y_size):
        pairs = [(i, (i + shift) % y_size) for i in range(y_size)]
        arrivals.append(lax.ppermute(parts, "y", pairs))
    by_y = jnp.take(jnp.stack(arrivals), (y_index - lax.iota(jnp.int32, y_size)) % y_size, axis=0)
    gathered = lax.all_gather(by_y, "z", axis=0, tiled=True)
    upper = gathered[:, peers:].transpose(1, 3, 0, 2).reshape(middle_count + top_count, width, columns)
    middle_result = upper[:middle_count]
    top_result = upper[middle_count:]
    node_result = lax.dynamic_index_in_dim(gathered, col_index, 1).transpose(1, 3, 0, 2).reshape(1, width, columns)

    parents = gathered[:, leaf_target].transpose(1, 0, 2, 3)
    leaf_result = leaf_backward(parents, leaf_solved, leaf_link, leaf_inverse)
    return (leaf_result, node_result, middle_result, top_result)


def solution(mesh):
    cores = len({d.core_on_chip for d in mesh.devices[:, 0]})
    y_size = len({d.coords[1] for d in mesh.devices[0]})
    grid = mesh.devices.reshape(mesh.shape["row"] // cores, cores, -1, y_size)
    view = Mesh(grid, ("x", "core", "z", "y"))
    placed = (
        P((*ROW, *COL), None, None),
        P((*ROW, *COL), None, None),
        P((*ROW, *COL), None, None),
        P((*ROW, *COL)),
        P((*ROW, *COL), None, None),
        P((*ROW, *COL), None, None),
        P((*ROW, *COL), None, None),
        P(ROW),
        P(ROW, None, None),
        P(ROW, None, None),
        P(ROW, None, None),
        P(ROW),
        P(),
        P(),
    )
    return jax.shard_map(
        local,
        mesh=view,
        in_specs=placed,
        out_specs=(
            P((*ROW, *COL), None, None),
            P((*ROW, *COL), None, None),
            P(ROW, None, None),
            P(),
        ),
        check_vma=False,
    )
```

```python
import jax
import jax.numpy as jnp
from jax import lax
from jax.experimental import pallas as pl
from jax.sharding import Mesh
from jax.sharding import PartitionSpec as P

ROW = ("x", "core")
COL = ("z", "y")


def apply_block(matrix, vectors):
    return jnp.einsum("nij,njr->nir", matrix, vectors, preferred_element_type=jnp.float32)


def apply_transposed(matrix, vectors):
    return jnp.einsum("nij,nir->njr", matrix, vectors, preferred_element_type=jnp.float32)


def piece_block(matrix, pieces):
    return jnp.einsum("nij,ncj->nci", matrix, pieces, preferred_element_type=jnp.float32)


def piece_transposed(matrix, pieces):
    return jnp.einsum("nij,nci->ncj", matrix, pieces, preferred_element_type=jnp.float32)


def slot_sums(targets, count, values):
    slots = lax.iota(jnp.int32, count)
    select = (slots[:, None] == targets[None, :]).astype(jnp.float32)
    return jnp.einsum("sk,k...->s...", select, values, precision=lax.Precision.HIGHEST)


def split_slot_sums(targets, count, values):
    slots = lax.iota(jnp.int32, count)
    select = (slots[:, None] == targets[None, :]).astype(jnp.bfloat16)
    high = values.astype(jnp.bfloat16)
    low = (values - high.astype(jnp.float32)).astype(jnp.bfloat16)
    total = jnp.einsum("sk,k...->s...", select, high, preferred_element_type=jnp.float32)
    return total + jnp.einsum("sk,k...->s...", select, low, preferred_element_type=jnp.float32)


def leaf_backward_kernel(parent_ref, solved_ref, link_t_ref, inverse_t_ref, out_ref):
    for k in range(parent_ref.shape[0]):
        pieces = parent_ref[k]
        parent_t = pieces.reshape(pieces.shape[0] * pieces.shape[1], pieces.shape[2])
        correction = lax.dot_general(
            link_t_ref[k], parent_t, (((1,), (1,)), ((), ())), preferred_element_type=jnp.float32
        )
        w = (solved_ref[k].astype(jnp.float32) - correction).astype(jnp.bfloat16)
        out_ref[k] = jnp.dot(inverse_t_ref[k], w, preferred_element_type=jnp.float32).astype(out_ref.dtype)


def leaf_backward(parents, leaf_solved, leaf_link, leaf_inverse):
    count, width, columns = leaf_solved.shape
    per_step = max(d for d in range(1, 13) if count % d == 0)
    pieces = parents.shape[1:]

    def own(step):
        return (step, 0, 0)

    cost = pl.CostEstimate(
        flops=4 * count * width * width * columns,
        transcendentals=0,
        bytes_accessed=2 * count * (3 * width * columns + 2 * width * width),
    )
    return pl.pallas_call(
        leaf_backward_kernel,
        grid=(count // per_step,),
        in_specs=[
            pl.BlockSpec((per_step, *pieces), lambda step: (step, 0, 0, 0)),
            pl.BlockSpec((per_step, width, columns), own),
            pl.BlockSpec((per_step, width, width), own),
            pl.BlockSpec((per_step, width, width), own),
        ],
        out_specs=pl.BlockSpec((per_step, width, columns), own),
        out_shape=jax.ShapeDtypeStruct(leaf_solved.shape, jnp.bfloat16),
        cost_estimate=cost,
    )(parents, leaf_solved, leaf_link.transpose(0, 2, 1), leaf_inverse.transpose(0, 2, 1))


def local(
    leaf_rhs,
    leaf_inverse,
    leaf_link,
    leaf_parent,
    node_rhs,
    node_inverse,
    node_link,
    node_parent,
    middle_rhs,
    middle_inverse,
    middle_link,
    middle_parent,
    top_rhs,
    top_inverse,
):
    y_size = lax.axis_size("y")
    z_size = lax.axis_size("z")
    peers = y_size * z_size
    col_index = lax.axis_index(COL)
    width = leaf_rhs.shape[1]
    columns = leaf_rhs.shape[2]
    chunk = columns // peers
    middle_count = middle_rhs.shape[0]
    top_count = top_rhs.shape[0]
    leaf_target = leaf_parent % peers
    middle_target = node_parent % middle_count
    start = col_index * chunk

    y_index = lax.axis_index("y")
    own_mats = jnp.concatenate([node_inverse, node_link], axis=0)
    mats = [own_mats]
    for shift in range(1, y_size):
        pairs = [(i, (i + shift) % y_size) for i in range(y_size)]
        mats.append(lax.ppermute(own_mats, "y", pairs))
    mats_by_y = jnp.take(jnp.stack(mats), (y_index - lax.iota(jnp.int32, y_size)) % y_size, axis=0)
    node_mats = lax.all_gather(mats_by_y, "z", axis=0, tiled=True)
    row_inverse = node_mats[:, 0]
    row_link = node_mats[:, 1]

    leaf_solved = apply_block(leaf_inverse, leaf_rhs).astype(jnp.bfloat16)
    leaf_update = jnp.einsum("kij,kjr->kri", leaf_link, leaf_solved, preferred_element_type=jnp.float32)
    half = peers // 2
    rhs_t = node_rhs.transpose(0, 2, 1)
    sums = []
    for group in range(2):
        targets = leaf_target - group * half
        entries = split_slot_sums(targets, half, leaf_update).astype(jnp.bfloat16)
        if group == 1:
            entries = jnp.concatenate([entries, rhs_t], axis=0)
        count = entries.shape[0]
        entries = entries.reshape(count, z_size, y_size, chunk, width).transpose(2, 1, 0, 3, 4)
        arrivals = [lax.dynamic_index_in_dim(entries, y_index, 0, keepdims=False)]
        for shift in range(1, y_size):
            outbound = lax.dynamic_index_in_dim(entries, (y_index + shift) % y_size, 0, keepdims=False)
            pairs = [(i, (i + shift) % y_size) for i in range(y_size)]
            arrivals.append(lax.ppermute(outbound, "y", pairs))
        partial = sum(a[:, :half].astype(jnp.float32) for a in arrivals).astype(jnp.bfloat16)
        if group == 1:
            partial = jnp.concatenate([partial, jnp.stack([a[:, half] for a in arrivals], axis=1)], axis=1)
        incoming = lax.all_to_all(partial, "z", 0, 0, tiled=True)
        sums.append(jnp.sum(incoming[:, :half].astype(jnp.float32), axis=0))
    node_sum = jnp.concatenate(sums, axis=0)
    offsets = (y_index - lax.iota(jnp.int32, y_size)) % y_size
    own_rhs = jnp.take(incoming[:, half:], offsets, axis=1).reshape(peers, chunk, width)
    node_y = (own_rhs.astype(jnp.float32) - node_sum).astype(jnp.bfloat16)
    node_solved = piece_block(row_inverse, node_y).astype(jnp.bfloat16)
    middle_sum = slot_sums(middle_target, middle_count, piece_block(row_link, node_solved))
    middle_piece = lax.dynamic_slice_in_dim(middle_rhs, start, chunk, 2).transpose(0, 2, 1)
    middle_y = (middle_piece.astype(jnp.float32) - middle_sum).astype(jnp.bfloat16)
    middle_solved = piece_block(middle_inverse, middle_y).astype(jnp.bfloat16)
    top_term = slot_sums(middle_parent, top_count, piece_block(middle_link, middle_solved))
    top_sum = top_term
    rows = lax.axis_size(ROW)
    step = 1
    while step < rows:
        top_sum = top_sum + lax.ppermute(top_sum, ROW, [(i, i ^ step) for i in range(rows)])
        step *= 2
    top_piece = lax.dynamic_slice_in_dim(top_rhs, start, chunk, 2).transpose(0, 2, 1)
    top_y = (top_piece.astype(jnp.float32) - top_sum).astype(jnp.bfloat16)
    top_solved = piece_block(top_inverse, top_y).astype(jnp.bfloat16)
    top_part = piece_transposed(top_inverse, top_solved).astype(jnp.bfloat16)
    middle_w = (
        middle_solved.astype(jnp.float32) - piece_transposed(middle_link, top_part[middle_parent])
    ).astype(jnp.bfloat16)
    middle_part = piece_transposed(middle_inverse, middle_w).astype(jnp.bfloat16)
    node_w = (
        node_solved.astype(jnp.float32) - piece_transposed(row_link, middle_part[middle_target])
    ).astype(jnp.bfloat16)
    node_part = piece_transposed(row_inverse, node_w).astype(jnp.bfloat16)

    parts = jnp.concatenate([node_part, middle_part, top_part], axis=0)
    arrivals = [parts]
    for shift in range(1, y_size):
        pairs = [(i, (i + shift) % y_size) for i in range(y_size)]
        arrivals.append(lax.ppermute(parts, "y", pairs))
    by_y = jnp.take(jnp.stack(arrivals), (y_index - lax.iota(jnp.int32, y_size)) % y_size, axis=0)
    gathered = lax.all_gather(by_y, "z", axis=0, tiled=True)
    upper = gathered[:, peers:].transpose(1, 3, 0, 2).reshape(middle_count + top_count, width, columns)
    middle_result = upper[:middle_count]
    top_result = upper[middle_count:]
    node_result = lax.dynamic_index_in_dim(gathered, col_index, 1).transpose(1, 3, 0, 2).reshape(1, width, columns)

    parents = gathered[:, leaf_target].transpose(1, 0, 2, 3)
    leaf_result = leaf_backward(parents, leaf_solved, leaf_link, leaf_inverse)
    return (leaf_result, node_result, middle_result, top_result)


def solution(mesh):
    cores = len({d.core_on_chip for d in mesh.devices[:, 0]})
    y_size = len({d.coords[1] for d in mesh.devices[0]})
    grid = mesh.devices.reshape(mesh.shape["row"] // cores, cores, -1, y_size)
    view = Mesh(grid, ("x", "core", "z", "y"))
    placed = (
        P((*ROW, *COL), None, None),
        P((*ROW, *COL), None, None),
        P((*ROW, *COL), None, None),
        P((*ROW, *COL)),
        P((*ROW, *COL), None, None),
        P((*ROW, *COL), None, None),
        P((*ROW, *COL), None, None),
        P(ROW),
        P(ROW, None, None),
        P(ROW, None, None),
        P(ROW, None, None),
        P(ROW),
        P(),
        P(),
    )
    return jax.shard_map(
        local,
        mesh=view,
        in_specs=placed,
        out_specs=(
            P((*ROW, *COL), None, None),
            P((*ROW, *COL), None, None),
            P(ROW, None, None),
            P(),
        ),
        check_vma=False,
    )
```
